128 devices in a mesh: frow: 16 (over y, z), fcol: 8 (over x, core).
Axes of the slice: x: 4, y: 4, z: 4, core: 2. Of those that a mesh axis runs over, the one named last changes fastest.
Arguments:
- front_orig: float32 [16, 1024, 8, 2048], P('frow', None, 'fcol'), may hold values from -0.1 to 45, as said below
- child_tiles: bfloat16 [8192, 128, 128], P(('frow', 'fcol')), may hold values from -0.25 to 0.25
- tile_target: int32 [8192, 2], P(('frow', 'fcol')), may hold values from 0 to 127, as said below
- tile_rows: int32 [8192, 128], P(('frow', 'fcol')), may hold values from 0 to 127, each once within a row
- tile_cols: int32 [8192, 128], P(('frow', 'fcol')), may hold values from 0 to 127, each once within a row
Outputs:
- front_out: float32 [16, 1024, 8, 2048], P('frow', None, 'fcol')
The draws below stay inside these ranges and needn't reach their ends.
Inputs may be any that keep to these rules, and one draw needn't show every extreme that they name: `front_orig`: Symmetric; the lower triangle of the front after every tile is added defines a positive definite matrix. `tile_target`: rows come 64 to a device in device order. Column 0 is the owner, frow index times 8 plus fcol index; column 1 the local block on that owner, local block row times 16 plus local block column; the block lies on or below the front's block diagonal. At most 2 tiles of one device go to one owner, and one owner receives exactly 2 from every device.
All inputs are finite; a program needn't handle non-finite values.
Results may differ from the reference program's by a relative error of at most 0.0003.
Values may be sent and summed in bfloat16 or wider, within the bound.
No kernel may reach another device: no remote copies, remote signals or barrier semaphores. Data moves between devices by JAX's collectives and lax.ppermute only.
A program may use at most 128 MiB of HBM per device.

```python
import math
import jax
import jax.numpy as jnp
from jax import lax

F = 16384
NB = 128
PW = 512
NPANEL = 2
TPD = 64
CAP = 2
ROWGRID = 16
COLGRID = 8
OWNERS = 128
LRB = 8
LCB = 16
TILES = 8192


def to_grid_drawn(natural):
    shaped = natural.reshape(LRB, ROWGRID, NB, LCB, COLGRID, NB)
    return shaped.transpose(1, 0, 2, 4, 3, 5).reshape(ROWGRID, LRB * NB, COLGRID, LCB * NB)


def draw_front_orig(key, part):
    noise_key, diag_key, scale_key = jax.random.split(jax.random.fold_in(key, 11), 3)
    noise_part = jnp.clip(0.01 * jax.random.normal(noise_key, (F, F), jnp.float32), -0.05, 0.05)
    scales = jnp.exp(jax.random.uniform(scale_key, (F,), jnp.float32, -0.35, 0.35))
    amplitude = 0.8
    grid_rows = F // NB
    row_ids = jnp.arange(grid_rows, dtype=jnp.float32)
    col_ids = jnp.arange(NB, dtype=jnp.float32)
    row_length = ROWGRID * 0.5
    col_length = NB * 0.125
    row_kernel = jnp.exp(-jnp.abs(row_ids[:, None] - row_ids[None, :]) / row_length)
    col_kernel = jnp.exp(-jnp.abs(col_ids[:, None] - col_ids[None, :]) / col_length)
    kernel = (row_kernel[:, None, :, None] * col_kernel[None, :, None, :]).reshape(F, F)
    coupled = amplitude * scales[:, None] * scales[None, :] * kernel
    symmetric = 0.5 * (noise_part + noise_part.T)
    diagonal = jnp.exp(jax.random.uniform(diag_key, (F,), jnp.float32, math.log(20.0), math.log(40.0)))
    on_diagonal = jnp.arange(F)[:, None] == jnp.arange(F)[None, :]
    full = coupled + jnp.where(on_diagonal, diagonal[None, :], symmetric)
    return to_grid_drawn(full).astype(jnp.float32)


def draw_child_tiles(key, part):
    tile_key = jax.random.fold_in(key, 23)
    values = jnp.clip(0.025 * jax.random.normal(tile_key, (TILES, NB, NB), jnp.float32), -0.15, 0.15)
    return values.astype(jnp.bfloat16)


def draw_tile_target(key, part):
    keys = jax.random.split(jax.random.fold_in(key, 37), 6)
    position_merit_aggregate = OWNERS * CAP
    random_perturbation = jax.random.randint(keys[0], (OWNERS, position_merit_aggregate), 0, 65536)
    pull_strength = jax.random.randint(keys[1], (OWNERS,), 0, 65536)
    favored_position_choice = jax.random.randint(keys[2], (), 0, OWNERS)
    position_numbers = jnp.arange(position_merit_aggregate, dtype=jnp.int32)
    position_occupant = position_numbers // CAP
    closeness_reward = jnp.where(position_occupant == favored_position_choice, 131072, 0)
    position_merits = (random_perturbation + jnp.take(pull_strength, position_occupant)[None, :] + closeness_reward[None, :]) * position_merit_aggregate + position_numbers[None, :]
    chosen = jax.lax.top_k(position_merits, TPD)[1]
    shuffle_keys = jax.random.split(keys[3], OWNERS)
    shuffles = jax.vmap(lambda sub_key: jax.random.permutation(sub_key, TPD))(shuffle_keys)
    chosen = jnp.take_along_axis(chosen, shuffles, axis=1)
    owner_of = (chosen // CAP).astype(jnp.int32)
    prow = owner_of // COLGRID
    pcol = owner_of % COLGRID
    col_most = jnp.minimum(LCB - 1, ((LRB - 1) * ROWGRID + prow - pcol) // COLGRID)
    col_pick = jax.random.randint(keys[4], owner_of.shape, 0, col_most + 1)
    row_least = jnp.maximum(0, -((prow - pcol - col_pick * COLGRID) // ROWGRID))
    row_pick = jax.random.randint(keys[5], owner_of.shape, row_least, LRB)
    block_of = row_pick * LCB + col_pick
    return jnp.stack([owner_of.reshape(-1), block_of.reshape(-1)], axis=1).astype(jnp.int32)


def setup_inputs(seed: int = 0) -> dict:
    splits = jax.random.split(jax.random.key(seed), 6)
    return {
        "front_orig": draw_front_orig(jax.random.fold_in(splits[5], 71), 0),
        "child_tiles": draw_child_tiles(jax.random.fold_in(splits[5], 71), 0),
        "tile_target": draw_tile_target(jax.random.fold_in(splits[5], 71), 0),
        "tile_rows": jax.vmap(lambda own: jax.random.permutation(own, NB))(jax.random.split(splits[3], TILES)).reshape((TILES, NB)).astype(jnp.int32),
        "tile_cols": jax.vmap(lambda own: jax.random.permutation(own, NB))(jax.random.split(splits[4], TILES)).reshape((TILES, NB)).astype(jnp.int32),
    }


def to_natural(grid_matrix):
    shaped = grid_matrix.reshape(ROWGRID, LRB, NB, COLGRID, LCB, NB)
    return shaped.transpose(1, 0, 2, 4, 3, 5).reshape(F, F)

def to_grid(natural):
    shaped = natural.reshape(LRB, ROWGRID, NB, LCB, COLGRID, NB)
    return shaped.transpose(1, 0, 2, 4, 3, 5).reshape(ROWGRID, LRB * NB, COLGRID, LCB * NB)

def reference(front_orig, child_tiles, tile_target, tile_rows, tile_cols):
    owner_of = tile_target[:, 0].astype(jnp.int32)
    block_of = tile_target[:, 1].astype(jnp.int32)
    block_row = block_of // LCB * ROWGRID + owner_of // COLGRID
    block_col = block_of % LCB * COLGRID + owner_of % COLGRID
    row_pos = (block_row[:, None] * NB + tile_rows).astype(jnp.int32)
    col_pos = (block_col[:, None] * NB + tile_cols).astype(jnp.int32)
    flat_pos = (row_pos[:, :, None] * F + col_pos[:, None, :]).reshape(-1).astype(jnp.int32)
    values = child_tiles.astype(jnp.float32).reshape(-1)
    matrix = to_natural(front_orig).reshape(-1).at[flat_pos].add(values).reshape(F, F)
    for panel_idx in range(NPANEL):
        start = panel_idx * PW
        stop = start + PW
        diag_block = matrix[start:stop, start:stop]
        symmetric = jnp.tril(diag_block) + jnp.tril(diag_block, -1).T
        factor = jnp.linalg.cholesky(symmetric)
        below = matrix[stop:, start:stop]
        solved = lax.linalg.triangular_solve(factor, below, left_side=False, lower=True, transpose_a=True)
        update = jnp.dot(solved.astype(jnp.float32), solved.T.astype(jnp.float32), precision=lax.Precision.HIGHEST, preferred_element_type=jnp.float32)
        matrix = matrix.at[stop:, stop:].add(-update)
        matrix = matrix.at[start:stop, start:stop].set(factor)
        matrix = matrix.at[stop:, start:stop].set(solved)
    return to_grid(jnp.tril(matrix))
```

```python
import jax
import jax.numpy as jnp
from jax import lax
from jax.sharding import PartitionSpec as P

PW = 512
NPANEL = 2
CAP = 2


def as_sent(x):
    return jax.tree.map(lambda a: a.astype(jnp.bfloat16) if a.dtype == jnp.float32 else a, x)


def broadcast(block, axis, source):
    block = jnp.where(lax.axis_index(axis) == source, block, jnp.zeros_like(block))
    return lax.psum(block, axis)


def place_tiles(received):
    tile_block, perm_block, target_block = received
    width = tile_block.shape[-1]
    positions = jnp.arange(width, dtype=jnp.int32)
    row_onehot = (perm_block[:, :, 0, None, :] == positions[:, None]).astype(jnp.bfloat16)
    col_onehot = (perm_block[:, :, 1, None, :] == positions[:, None]).astype(jnp.bfloat16)
    moved = jnp.einsum(
        "abxi,abij->abxj", row_onehot, tile_block, preferred_element_type=jnp.float32
    ).astype(jnp.bfloat16)
    placed = jnp.einsum(
        "abxj,abyj->abxy", moved, col_onehot, preferred_element_type=jnp.float32
    ).astype(jnp.bfloat16)
    return (placed, target_block)


def subtract_product(matrix, row_factor, col_factor):
    product = jnp.dot(
        row_factor,
        col_factor.T,
        precision=lax.Precision.HIGHEST,
        preferred_element_type=jnp.float32,
    )
    return matrix - product


def shards(front_orig, child_tiles, tile_target, tile_rows, tile_cols):
    row_devs = lax.axis_size("frow")
    col_devs = lax.axis_size("fcol")
    owners = row_devs * col_devs
    row_here = lax.axis_index("frow")
    col_here = lax.axis_index("fcol")
    width = child_tiles.shape[1]
    held = child_tiles.shape[0]
    slot_count = owners * CAP
    owner_of = tile_target[:, 0]
    block_of = tile_target[:, 1]
    tile_order = jnp.arange(held, dtype=jnp.int32)
    same_owner = owner_of[:, None] == owner_of[None, :]
    earlier = tile_order[None, :] < tile_order[:, None]
    rank_of = jnp.sum(jnp.where(same_owner & earlier, 1, 0), axis=1).astype(jnp.int32)
    slot_of = owner_of * CAP + rank_of
    slot_match = slot_of[None, :] == jnp.arange(slot_count, dtype=jnp.int32)[:, None]
    source_tile = jnp.sum(jnp.where(slot_match, tile_order[None, :], 0), axis=1)
    filled = jnp.any(slot_match, axis=1)
    send_tiles = jnp.where(
        filled[:, None, None],
        jnp.take(child_tiles, source_tile, axis=0),
        jnp.zeros((), jnp.bfloat16),
    )
    send_perms = jnp.stack(
        [jnp.take(tile_rows, source_tile, axis=0), jnp.take(tile_cols, source_tile, axis=0)], axis=1
    )
    send_blocks = jnp.take(block_of, source_tile, axis=0)
    placed, blocks_in = place_tiles(
        (
            lax.all_to_all(
                send_tiles.reshape(owners, CAP, width, width),
                ("frow", "fcol"),
                split_axis=0,
                concat_axis=0,
                tiled=True,
            ),
            lax.all_to_all(
                send_perms.reshape(owners, CAP, 2, width),
                ("frow", "fcol"),
                split_axis=0,
                concat_axis=0,
                tiled=True,
            ),
            lax.all_to_all(
                send_blocks.reshape(owners, CAP),
                ("frow", "fcol"),
                split_axis=0,
                concat_axis=0,
                tiled=True,
            ),
        )
    )
    local = front_orig[0, :, 0, :]
    row_blocks = local.shape[0] // width
    col_blocks = local.shape[1] // width
    block_ids = jnp.arange(row_blocks * col_blocks, dtype=jnp.int32)
    block_onehot = (blocks_in.reshape(1, slot_count) == block_ids[:, None]).astype(jnp.bfloat16)
    summed = jnp.dot(
        block_onehot, placed.reshape(slot_count, width * width), preferred_element_type=jnp.float32
    )
    added = (
        summed.reshape(row_blocks, col_blocks, width, width)
        .transpose(0, 2, 1, 3)
        .reshape(local.shape)
    )
    matrix = local + added
    local_rows = jnp.arange(local.shape[0], dtype=jnp.int32)
    local_cols = jnp.arange(local.shape[1], dtype=jnp.int32)
    global_rows = (local_rows // width * row_devs + row_here) * width + local_rows % width
    global_cols = (local_cols // width * col_devs + col_here) * width + local_cols % width
    total = NPANEL * PW
    hi = lax.Precision.HIGHEST
    row_panel = lax.all_gather(
        matrix[:, :width].astype(jnp.bfloat16), "fcol", axis=1, tiled=True
    )[:, :total]
    half = row_devs // col_devs
    perms = []
    for shift in range(half):
        pairs = []
        for src_row in range(row_devs):
            for src_col in range(col_devs):
                part = src_row // col_devs
                dst_row = ((part + shift) % half) * col_devs + src_col
                dst_col = src_row % col_devs
                pairs.append((src_row * col_devs + src_col, dst_row * col_devs + dst_col))
        perms.append(pairs)
    got = [lax.ppermute(row_panel, ("frow", "fcol"), perm) for perm in perms]
    my_part = row_here // col_devs
    ordered = []
    for part in range(half):
        pick = got[0]
        for shift in range(1, half):
            pick = jnp.where((my_part - shift) % half == part, got[shift], pick)
        if half == 1:
            pick = got[0]
        ordered.append(pick.reshape(row_blocks, width, total))
    col_panel = jnp.stack(ordered, axis=1).reshape(local.shape[1], total)
    corner_blocks = total // width
    first = matrix[:width, :width].astype(jnp.bfloat16)
    every = lax.all_gather(first, ("frow", "fcol"), axis=0, tiled=False)
    every = every.reshape(row_devs, col_devs, width, width)[:corner_blocks, :corner_blocks]
    corner = every.transpose(0, 2, 1, 3).reshape(total, total).astype(jnp.float32)
    rows_all = jnp.concatenate([row_panel, col_panel], axis=0).astype(jnp.float32)
    n_own = local.shape[0]
    factor_full = jnp.zeros((total, total), jnp.float32)
    pieces = []
    eye = jnp.eye(PW, dtype=jnp.float32)
    for panel_idx in range(NPANEL):
        start = panel_idx * PW
        stop = start + PW
        diag_block = corner[start:stop, start:stop]
        symmetric = jnp.tril(diag_block) + jnp.tril(diag_block, -1).T
        factor = jnp.linalg.cholesky(symmetric)
        inverse = lax.linalg.triangular_solve(factor, eye, left_side=True, lower=True)
        factor_full = factor_full.at[start:stop, start:stop].set(factor)
        solved_rows = jnp.dot(
            rows_all[:, start:stop], inverse.T, precision=hi, preferred_element_type=jnp.float32
        )
        pieces.append(solved_rows)
        if stop < total:
            below = jnp.dot(
                corner[stop:, start:stop], inverse.T, precision=hi, preferred_element_type=jnp.float32
            )
            factor_full = factor_full.at[stop:, start:stop].set(below)
            corner = corner.at[stop:, stop:].add(
                -jnp.dot(below, below.T, precision=hi, preferred_element_type=jnp.float32)
            )
            rows_all = rows_all.at[:, stop:].add(
                -jnp.dot(solved_rows, below.T, precision=hi, preferred_element_type=jnp.float32)
            )
    solved = jnp.concatenate(pieces, axis=1)
    row_factor = solved[:n_own]
    col_factor = solved[n_own:]
    matrix = subtract_product(matrix, row_factor, col_factor)
    in_corner = (global_rows < total)[:, None]
    corner_rows = jnp.take(factor_full, jnp.clip(global_rows, 0, total - 1), axis=0)
    panel_vals = jnp.where(in_corner, corner_rows, row_factor)
    own_part = lax.dynamic_slice_in_dim(panel_vals, col_here * width, width, axis=1)
    matrix = matrix.at[:, :width].set(own_part)
    lower_part = global_rows[:, None] >= global_cols[None, :]
    result = jnp.where(lower_part, matrix, 0.0)
    return result[None, :, None, :]


def solution(mesh):
    return jax.shard_map(
        shards,
        mesh=mesh,
        in_specs=(
            P("frow", None, "fcol", None),
            P(("frow", "fcol"), None, None),
            P(("frow", "fcol"), None),
            P(("frow", "fcol"), None),
            P(("frow", "fcol"), None),
        ),
        out_specs=P("frow", None, "fcol", None),
        check_vma=False,
    )
```

```python
import jax
import jax.numpy as jnp
from jax import lax
from jax.sharding import PartitionSpec as P

PW = 512
NPANEL = 2
CAP = 2


def as_sent(x):
    return jax.tree.map(lambda a: a.astype(jnp.bfloat16) if a.dtype == jnp.float32 else a, x)


def broadcast(block, axis, source):
    block = jnp.where(lax.axis_index(axis) == source, block, jnp.zeros_like(block))
    return lax.psum(block, axis)


def place_tiles(received):
    tile_block, perm_block, target_block = received
    width = tile_block.shape[-1]
    positions = jnp.arange(width, dtype=jnp.int32)
    row_onehot = (perm_block[:, :, 0, None, :] == positions[:, None]).astype(jnp.bfloat16)
    col_onehot = (perm_block[:, :, 1, None, :] == positions[:, None]).astype(jnp.bfloat16)
    moved = jnp.einsum(
        "abxi,abij->abxj", row_onehot, tile_block, preferred_element_type=jnp.float32
    ).astype(jnp.bfloat16)
    placed = jnp.einsum(
        "abxj,abyj->abxy", moved, col_onehot, preferred_element_type=jnp.float32
    ).astype(jnp.bfloat16)
    return (placed, target_block)


def subtract_product(matrix, row_factor, col_factor):
    product = jnp.dot(
        row_factor,
        col_factor.T,
        precision=lax.Precision.HIGHEST,
        preferred_element_type=jnp.float32,
    )
    return matrix - product


def shards(front_orig, child_tiles, tile_target, tile_rows, tile_cols):
    row_devs = lax.axis_size("frow")
    col_devs = lax.axis_size("fcol")
    owners = row_devs * col_devs
    row_here = lax.axis_index("frow")
    col_here = lax.axis_index("fcol")
    width = child_tiles.shape[1]
    held = child_tiles.shape[0]
    slot_count = owners * CAP
    owner_of = tile_target[:, 0]
    block_of = tile_target[:, 1]
    tile_order = jnp.arange(held, dtype=jnp.int32)
    same_owner = owner_of[:, None] == owner_of[None, :]
    earlier = tile_order[None, :] < tile_order[:, None]
    rank_of = jnp.sum(jnp.where(same_owner & earlier, 1, 0), axis=1).astype(jnp.int32)
    slot_of = owner_of * CAP + rank_of
    slot_match = slot_of[None, :] == jnp.arange(slot_count, dtype=jnp.int32)[:, None]
    source_tile = jnp.sum(jnp.where(slot_match, tile_order[None, :], 0), axis=1)
    filled = jnp.any(slot_match, axis=1)
    send_tiles = jnp.where(
        filled[:, None, None],
        jnp.take(child_tiles, source_tile, axis=0),
        jnp.zeros((), jnp.bfloat16),
    )
    send_perms = jnp.stack(
        [jnp.take(tile_rows, source_tile, axis=0), jnp.take(tile_cols, source_tile, axis=0)], axis=1
    )
    send_blocks = jnp.take(block_of, source_tile, axis=0)
    placed, blocks_in = place_tiles(
        (
            lax.all_to_all(
                send_tiles.reshape(owners, CAP, width, width),
                ("frow", "fcol"),
                split_axis=0,
                concat_axis=0,
                tiled=True,
            ),
            lax.all_to_all(
                send_perms.reshape(owners, CAP, 2, width),
                ("frow", "fcol"),
                split_axis=0,
                concat_axis=0,
                tiled=True,
            ),
            lax.all_to_all(
                send_blocks.reshape(owners, CAP),
                ("frow", "fcol"),
                split_axis=0,
                concat_axis=0,
                tiled=True,
            ),
        )
    )
    local = front_orig[0, :, 0, :]
    row_blocks = local.shape[0] // width
    col_blocks = local.shape[1] // width
    block_ids = jnp.arange(row_blocks * col_blocks, dtype=jnp.int32)
    block_onehot = (blocks_in.reshape(1, slot_count) == block_ids[:, None]).astype(jnp.bfloat16)
    summed = jnp.dot(
        block_onehot, placed.reshape(slot_count, width * width), preferred_element_type=jnp.float32
    )
    added = (
        summed.reshape(row_blocks, col_blocks, width, width)
        .transpose(0, 2, 1, 3)
        .reshape(local.shape)
    )
    matrix = local + added
    local_rows = jnp.arange(local.shape[0], dtype=jnp.int32)
    local_cols = jnp.arange(local.shape[1], dtype=jnp.int32)
    global_rows = (local_rows // width * row_devs + row_here) * width + local_rows % width
    global_cols = (local_cols // width * col_devs + col_here) * width + local_cols % width
    total = NPANEL * PW
    hi = lax.Precision.HIGHEST
    row_panel = lax.all_gather(
        matrix[:, :width].astype(jnp.bfloat16), "fcol", axis=1, tiled=True
    )[:, :total]
    half = row_devs // col_devs
    pairs = []
    for src_row in range(row_devs):
        for src_col in range(col_devs):
            dst_row = (src_row // col_devs) * col_devs + src_col
            dst_col = src_row % col_devs
            pairs.append((src_row * col_devs + src_col, dst_row * col_devs + dst_col))
    piece = lax.dynamic_slice_in_dim(row_panel, col_here * width, width, axis=0)
    piece = lax.ppermute(piece, ("frow", "fcol"), pairs)
    col_all = lax.all_gather(piece, "frow", axis=0, tiled=False)
    col_panel = (
        col_all.reshape(half, row_blocks, width, total)
        .transpose(1, 0, 2, 3)
        .reshape(local.shape[1], total)
    )
    corner_blocks = total // width
    first = matrix[:width, :width].astype(jnp.bfloat16)
    every = lax.all_gather(first, ("frow", "fcol"), axis=0, tiled=False)
    every = every.reshape(row_devs, col_devs, width, width)[:corner_blocks, :corner_blocks]
    corner = every.transpose(0, 2, 1, 3).reshape(total, total).astype(jnp.float32)
    rows_all = jnp.concatenate([row_panel, col_panel], axis=0).astype(jnp.float32)
    n_own = local.shape[0]
    factor_full = jnp.zeros((total, total), jnp.float32)
    pieces = []
    eye = jnp.eye(PW, dtype=jnp.float32)
    for panel_idx in range(NPANEL):
        start = panel_idx * PW
        stop = start + PW
        diag_block = corner[start:stop, start:stop]
        symmetric = jnp.tril(diag_block) + jnp.tril(diag_block, -1).T
        factor = jnp.linalg.cholesky(symmetric)
        inverse = lax.linalg.triangular_solve(factor, eye, left_side=True, lower=True)
        factor_full = factor_full.at[start:stop, start:stop].set(factor)
        solved_rows = jnp.dot(
            rows_all[:, start:stop], inverse.T, precision=hi, preferred_element_type=jnp.float32
        )
        pieces.append(solved_rows)
        if stop < total:
            below = jnp.dot(
                corner[stop:, start:stop], inverse.T, precision=hi, preferred_element_type=jnp.float32
            )
            factor_full = factor_full.at[stop:, start:stop].set(below)
            corner = corner.at[stop:, stop:].add(
                -jnp.dot(below, below.T, precision=hi, preferred_element_type=jnp.float32)
            )
            rows_all = rows_all.at[:, stop:].add(
                -jnp.dot(solved_rows, below.T, precision=hi, preferred_element_type=jnp.float32)
            )
    solved = jnp.concatenate(pieces, axis=1)
    row_factor = solved[:n_own]
    col_factor = solved[n_own:]
    matrix = subtract_product(matrix, row_factor, col_factor)
    in_corner = (global_rows < total)[:, None]
    corner_rows = jnp.take(factor_full, jnp.clip(global_rows, 0, total - 1), axis=0)
    panel_vals = jnp.where(in_corner, corner_rows, row_factor)
    own_part = lax.dynamic_slice_in_dim(panel_vals, col_here * width, width, axis=1)
    matrix = matrix.at[:, :width].set(own_part)
    lower_part = global_rows[:, None] >= global_cols[None, :]
    result = jnp.where(lower_part, matrix, 0.0)
    return result[None, :, None, :]


def solution(mesh):
    return jax.shard_map(
        shards,
        mesh=mesh,
        in_specs=(
            P("frow", None, "fcol", None),
            P(("frow", "fcol"), None, None),
            P(("frow", "fcol"), None),
            P(("frow", "fcol"), None),
            P(("frow", "fcol"), None),
        ),
        out_specs=P("frow", None, "fcol", None),
        check_vma=False,
    )
```

```python
import jax
import jax.numpy as jnp
from jax import lax
from jax.sharding import PartitionSpec as P

PW = 512
NPANEL = 2
CAP = 2


def as_sent(x):
    return jax.tree.map(lambda a: a.astype(jnp.bfloat16) if a.dtype == jnp.float32 else a, x)


def broadcast(block, axis, source):
    block = jnp.where(lax.axis_index(axis) == source, block, jnp.zeros_like(block))
    return lax.psum(block, axis)


def place_tiles(received):
    tile_block, perm_block, target_block = received
    width = tile_block.shape[-1]
    positions = jnp.arange(width, dtype=jnp.int32)
    row_onehot = (perm_block[:, :, 0, None, :] == positions[:, None]).astype(jnp.bfloat16)
    col_onehot = (perm_block[:, :, 1, None, :] == positions[:, None]).astype(jnp.bfloat16)
    moved = jnp.einsum(
        "abxi,abij->abxj", row_onehot, tile_block, preferred_element_type=jnp.float32
    ).astype(jnp.bfloat16)
    placed = jnp.einsum(
        "abxj,abyj->abxy", moved, col_onehot, preferred_element_type=jnp.float32
    ).astype(jnp.bfloat16)
    return (placed, target_block)


def subtract_product(matrix, row_factor, col_factor):
    product = jnp.dot(
        row_factor,
        col_factor.T,
        precision=lax.Precision.HIGHEST,
        preferred_element_type=jnp.float32,
    )
    return matrix - product


def shards(front_orig, child_tiles, tile_target, tile_rows, tile_cols):
    row_devs = lax.axis_size("frow")
    col_devs = lax.axis_size("fcol")
    owners = row_devs * col_devs
    row_here = lax.axis_index("frow")
    col_here = lax.axis_index("fcol")
    width = child_tiles.shape[1]
    held = child_tiles.shape[0]
    slot_count = owners * CAP
    owner_of = tile_target[:, 0]
    block_of = tile_target[:, 1]
    tile_order = jnp.arange(held, dtype=jnp.int32)
    same_owner = owner_of[:, None] == owner_of[None, :]
    earlier = tile_order[None, :] < tile_order[:, None]
    rank_of = jnp.sum(jnp.where(same_owner & earlier, 1, 0), axis=1).astype(jnp.int32)
    slot_of = owner_of * CAP + rank_of
    slot_match = slot_of[None, :] == jnp.arange(slot_count, dtype=jnp.int32)[:, None]
    source_tile = jnp.sum(jnp.where(slot_match, tile_order[None, :], 0), axis=1)
    filled = jnp.any(slot_match, axis=1)
    own_perms = jnp.stack([tile_rows, tile_cols], axis=1)
    placed_here, _ = place_tiles((child_tiles[None], own_perms[None], block_of[None]))
    placed_here = placed_here[0]
    send_tiles = jnp.where(
        filled[:, None, None],
        jnp.take(placed_here, source_tile, axis=0),
        jnp.zeros((), jnp.bfloat16),
    )
    send_blocks = jnp.where(filled, jnp.take(block_of, source_tile, axis=0), -1)
    placed = lax.all_to_all(
        send_tiles.reshape(owners, CAP, width, width),
        ("frow", "fcol"),
        split_axis=0,
        concat_axis=0,
        tiled=True,
    )
    blocks_in = lax.all_to_all(
        send_blocks.reshape(owners, CAP),
        ("frow", "fcol"),
        split_axis=0,
        concat_axis=0,
        tiled=True,
    )
    local = front_orig[0, :, 0, :]
    row_blocks = local.shape[0] // width
    col_blocks = local.shape[1] // width
    block_ids = jnp.arange(row_blocks * col_blocks, dtype=jnp.int32)
    block_onehot = (blocks_in.reshape(1, slot_count) == block_ids[:, None]).astype(jnp.bfloat16)
    summed = jnp.dot(
        block_onehot, placed.reshape(slot_count, width * width), preferred_element_type=jnp.float32
    )
    added = (
        summed.reshape(row_blocks, col_blocks, width, width)
        .transpose(0, 2, 1, 3)
        .reshape(local.shape)
    )
    matrix = local + added
    local_rows = jnp.arange(local.shape[0], dtype=jnp.int32)
    local_cols = jnp.arange(local.shape[1], dtype=jnp.int32)
    global_rows = (local_rows // width * row_devs + row_here) * width + local_rows % width
    global_cols = (local_cols // width * col_devs + col_here) * width + local_cols % width
    total = NPANEL * PW
    hi = lax.Precision.HIGHEST
    row_panel = lax.all_gather(
        matrix[:, :width].astype(jnp.bfloat16), "fcol", axis=1, tiled=True
    )[:, :total]
    half = row_devs // col_devs
    pairs = []
    for src_row in range(row_devs):
        for src_col in range(col_devs):
            dst_row = (src_row // col_devs) * col_devs + src_col
            dst_col = src_row % col_devs
            pairs.append((src_row * col_devs + src_col, dst_row * col_devs + dst_col))
    piece = lax.dynamic_slice_in_dim(row_panel, col_here * width, width, axis=0)
    piece = lax.ppermute(piece, ("frow", "fcol"), pairs)
    col_all = lax.all_gather(piece, "frow", axis=0, tiled=False)
    col_panel = (
        col_all.reshape(half, row_blocks, width, total)
        .transpose(1, 0, 2, 3)
        .reshape(local.shape[1], total)
    )
    corner_blocks = total // width
    first = matrix[:width, :width].astype(jnp.bfloat16)
    every = lax.all_gather(first, ("frow", "fcol"), axis=0, tiled=False)
    every = every.reshape(row_devs, col_devs, width, width)[:corner_blocks, :corner_blocks]
    corner = every.transpose(0, 2, 1, 3).reshape(total, total).astype(jnp.float32)
    rows_all = jnp.concatenate([row_panel, col_panel], axis=0).astype(jnp.float32)
    n_own = local.shape[0]
    factor_full = jnp.zeros((total, total), jnp.float32)
    pieces = []
    eye = jnp.eye(PW, dtype=jnp.float32)
    for panel_idx in range(NPANEL):
        start = panel_idx * PW
        stop = start + PW
        diag_block = corner[start:stop, start:stop]
        symmetric = jnp.tril(diag_block) + jnp.tril(diag_block, -1).T
        factor = jnp.linalg.cholesky(symmetric)
        inverse = lax.linalg.triangular_solve(factor, eye, left_side=True, lower=True)
        factor_full = factor_full.at[start:stop, start:stop].set(factor)
        solved_rows = jnp.dot(
            rows_all[:, start:stop], inverse.T, precision=hi, preferred_element_type=jnp.float32
        )
        pieces.append(solved_rows)
        if stop < total:
            below = jnp.dot(
                corner[stop:, start:stop], inverse.T, precision=hi, preferred_element_type=jnp.float32
            )
            factor_full = factor_full.at[stop:, start:stop].set(below)
            corner = corner.at[stop:, stop:].add(
                -jnp.dot(below, below.T, precision=hi, preferred_element_type=jnp.float32)
            )
            rows_all = rows_all.at[:, stop:].add(
                -jnp.dot(solved_rows, below.T, precision=hi, preferred_element_type=jnp.float32)
            )
    solved = jnp.concatenate(pieces, axis=1)
    row_factor = solved[:n_own]
    col_factor = solved[n_own:]
    matrix = subtract_product(matrix, row_factor, col_factor)
    in_corner = (global_rows < total)[:, None]
    corner_rows = jnp.take(factor_full, jnp.clip(global_rows, 0, total - 1), axis=0)
    panel_vals = jnp.where(in_corner, corner_rows, row_factor)
    own_part = lax.dynamic_slice_in_dim(panel_vals, col_here * width, width, axis=1)
    matrix = matrix.at[:, :width].set(own_part)
    lower_part = global_rows[:, None] >= global_cols[None, :]
    result = jnp.where(lower_part, matrix, 0.0)
    return result[None, :, None, :]


def solution(mesh):
    return jax.shard_map(
        shards,
        mesh=mesh,
        in_specs=(
            P("frow", None, "fcol", None),
            P(("frow", "fcol"), None, None),
            P(("frow", "fcol"), None),
            P(("frow", "fcol"), None),
            P(("frow", "fcol"), None),
        ),
        out_specs=P("frow", None, "fcol", None),
        check_vma=False,
    )
```

```python
import jax
import jax.numpy as jnp
from jax import lax
from jax.sharding import PartitionSpec as P

PW = 512
NPANEL = 2
CAP = 2


def as_sent(x):
    return jax.tree.map(lambda a: a.astype(jnp.bfloat16) if a.dtype == jnp.float32 else a, x)


def broadcast(block, axis, source):
    block = jnp.where(lax.axis_index(axis) == source, block, jnp.zeros_like(block))
    return lax.psum(block, axis)


def place_tiles(received):
    tile_block, perm_block, target_block = received
    width = tile_block.shape[-1]
    positions = jnp.arange(width, dtype=jnp.int32)
    row_onehot = (perm_block[:, :, 0, None, :] == positions[:, None]).astype(jnp.bfloat16)
    col_onehot = (perm_block[:, :, 1, None, :] == positions[:, None]).astype(jnp.bfloat16)
    moved = jnp.einsum(
        "abxi,abij->abxj", row_onehot, tile_block, preferred_element_type=jnp.float32
    ).astype(jnp.bfloat16)
    placed = jnp.einsum(
        "abxj,abyj->abxy", moved, col_onehot, preferred_element_type=jnp.float32
    ).astype(jnp.bfloat16)
    return (placed, target_block)


def subtract_product(matrix, row_factor, col_factor):
    product = jnp.dot(
        row_factor,
        col_factor.T,
        precision=lax.Precision.HIGH,
        preferred_element_type=jnp.float32,
    )
    return matrix - product


def shards(front_orig, child_tiles, tile_target, tile_rows, tile_cols):
    row_devs = lax.axis_size("frow")
    col_devs = lax.axis_size("fcol")
    owners = row_devs * col_devs
    row_here = lax.axis_index("frow")
    col_here = lax.axis_index("fcol")
    width = child_tiles.shape[1]
    held = child_tiles.shape[0]
    slot_count = owners * CAP
    owner_of = tile_target[:, 0]
    block_of = tile_target[:, 1]
    tile_order = jnp.arange(held, dtype=jnp.int32)
    same_owner = owner_of[:, None] == owner_of[None, :]
    earlier = tile_order[None, :] < tile_order[:, None]
    rank_of = jnp.sum(jnp.where(same_owner & earlier, 1, 0), axis=1).astype(jnp.int32)
    slot_of = owner_of * CAP + rank_of
    slot_match = slot_of[None, :] == jnp.arange(slot_count, dtype=jnp.int32)[:, None]
    source_tile = jnp.sum(jnp.where(slot_match, tile_order[None, :], 0), axis=1)
    filled = jnp.any(slot_match, axis=1)
    own_perms = jnp.stack([tile_rows, tile_cols], axis=1)
    placed_here, _ = place_tiles((child_tiles[None], own_perms[None], block_of[None]))
    placed_here = placed_here[0]
    send_tiles = jnp.where(
        filled[:, None, None],
        jnp.take(placed_here, source_tile, axis=0),
        jnp.zeros((), jnp.bfloat16),
    )
    send_blocks = jnp.where(filled, jnp.take(block_of, source_tile, axis=0), -1)
    placed = lax.all_to_all(
        send_tiles.reshape(owners, CAP, width, width),
        ("frow", "fcol"),
        split_axis=0,
        concat_axis=0,
        tiled=True,
    )
    blocks_in = lax.all_to_all(
        send_blocks.reshape(owners, CAP),
        ("frow", "fcol"),
        split_axis=0,
        concat_axis=0,
        tiled=True,
    )
    local = front_orig[0, :, 0, :]
    row_blocks = local.shape[0] // width
    col_blocks = local.shape[1] // width
    block_ids = jnp.arange(row_blocks * col_blocks, dtype=jnp.int32)
    block_onehot = (blocks_in.reshape(1, slot_count) == block_ids[:, None]).astype(jnp.bfloat16)
    summed = jnp.dot(
        block_onehot, placed.reshape(slot_count, width * width), preferred_element_type=jnp.float32
    )
    added = (
        summed.reshape(row_blocks, col_blocks, width, width)
        .transpose(0, 2, 1, 3)
        .reshape(local.shape)
    )
    matrix = local + added
    local_rows = jnp.arange(local.shape[0], dtype=jnp.int32)
    local_cols = jnp.arange(local.shape[1], dtype=jnp.int32)
    global_rows = (local_rows // width * row_devs + row_here) * width + local_rows % width
    global_cols = (local_cols // width * col_devs + col_here) * width + local_cols % width
    total = NPANEL * PW
    hi = lax.Precision.HIGH

    corner_blocks = total // width
    first = matrix[:width, :width].astype(jnp.bfloat16)
    every = lax.all_gather(first, ("frow", "fcol"), axis=0, tiled=False)
    every, own_column = lax.optimization_barrier((every, matrix[:, :width]))
    every = every.reshape(row_devs, col_devs, width, width)[:corner_blocks, :corner_blocks]
    corner = every.transpose(0, 2, 1, 3).reshape(total, total).astype(jnp.float32)
    row_panel = lax.all_gather(
        own_column.astype(jnp.bfloat16), "fcol", axis=1, tiled=True
    )[:, :total]
    half = row_devs // col_devs
    pairs = []
    for src_row in range(row_devs):
        for src_col in range(col_devs):
            dst_row = (src_row // col_devs) * col_devs + src_col
            dst_col = src_row % col_devs
            pairs.append((src_row * col_devs + src_col, dst_row * col_devs + dst_col))
    piece = lax.dynamic_slice_in_dim(row_panel, col_here * width, width, axis=0)
    piece = lax.ppermute(piece, ("frow", "fcol"), pairs)
    col_all = lax.all_gather(piece, "frow", axis=0, tiled=False)
    col_panel = (
        col_all.reshape(half, row_blocks, width, total)
        .transpose(1, 0, 2, 3)
        .reshape(local.shape[1], total)
    )
    rows_all = jnp.concatenate([row_panel, col_panel], axis=0).astype(jnp.float32)
    n_own = local.shape[0]
    factor_full = jnp.zeros((total, total), jnp.float32)
    pieces = []
    eye = jnp.eye(PW, dtype=jnp.float32)
    for panel_idx in range(NPANEL):
        start = panel_idx * PW
        stop = start + PW
        diag_block = corner[start:stop, start:stop]
        symmetric = jnp.tril(diag_block) + jnp.tril(diag_block, -1).T
        factor = jnp.linalg.cholesky(symmetric)
        inverse = lax.linalg.triangular_solve(factor, eye, left_side=True, lower=True)
        factor_full = factor_full.at[start:stop, start:stop].set(factor)
        solved_rows = jnp.dot(
            rows_all[:, start:stop], inverse.T, precision=hi, preferred_element_type=jnp.float32
        )
        pieces.append(solved_rows)
        if stop < total:
            below = jnp.dot(
                corner[stop:, start:stop], inverse.T, precision=hi, preferred_element_type=jnp.float32
            )
            factor_full = factor_full.at[stop:, start:stop].set(below)
            corner = corner.at[stop:, stop:].add(
                -jnp.dot(below, below.T, precision=hi, preferred_element_type=jnp.float32)
            )
            rows_all = rows_all.at[:, stop:].add(
                -jnp.dot(solved_rows, below.T, precision=hi, preferred_element_type=jnp.float32)
            )
    solved = jnp.concatenate(pieces, axis=1)
    row_factor = solved[:n_own]
    col_factor = solved[n_own:]
    matrix = subtract_product(matrix, row_factor, col_factor)
    in_corner = (global_rows < total)[:, None]
    corner_rows = jnp.take(factor_full, jnp.clip(global_rows, 0, total - 1), axis=0)
    panel_vals = jnp.where(in_corner, corner_rows, row_factor)
    own_part = lax.dynamic_slice_in_dim(panel_vals, col_here * width, width, axis=1)
    matrix = matrix.at[:, :width].set(own_part)
    lower_part = global_rows[:, None] >= global_cols[None, :]
    result = jnp.where(lower_part, matrix, 0.0)
    return result[None, :, None, :]


def solution(mesh):
    return jax.shard_map(
        shards,
        mesh=mesh,
        in_specs=(
            P("frow", None, "fcol", None),
            P(("frow", "fcol"), None, None),
            P(("frow", "fcol"), None),
            P(("frow", "fcol"), None),
            P(("frow", "fcol"), None),
        ),
        out_specs=P("frow", None, "fcol", None),
        check_vma=False,
    )
```

```python
import jax
import jax.numpy as jnp
from jax import lax
from jax.sharding import PartitionSpec as P

PW = 512
NPANEL = 2
CAP = 2


def as_sent(x):
    return jax.tree.map(lambda a: a.astype(jnp.bfloat16) if a.dtype == jnp.float32 else a, x)


def broadcast(block, axis, source):
    block = jnp.where(lax.axis_index(axis) == source, block, jnp.zeros_like(block))
    return lax.psum(block, axis)


def place_tiles(received):
    tile_block, perm_block, target_block = received
    width = tile_block.shape[-1]
    positions = jnp.arange(width, dtype=jnp.int32)
    row_onehot = (perm_block[:, :, 0, None, :] == positions[:, None]).astype(jnp.bfloat16)
    col_onehot = (perm_block[:, :, 1, None, :] == positions[:, None]).astype(jnp.bfloat16)
    moved = jnp.einsum(
        "abxi,abij->abxj", row_onehot, tile_block, preferred_element_type=jnp.float32
    ).astype(jnp.bfloat16)
    placed = jnp.einsum(
        "abxj,abyj->abxy", moved, col_onehot, preferred_element_type=jnp.float32
    ).astype(jnp.bfloat16)
    return (placed, target_block)


def subtract_product(matrix, row_factor, col_factor):
    product = jnp.dot(
        row_factor,
        col_factor.T,
        precision=lax.Precision.HIGH,
        preferred_element_type=jnp.float32,
    )
    return matrix - product


def shards(front_orig, child_tiles, tile_target, tile_rows, tile_cols):
    row_devs = lax.axis_size("frow")
    col_devs = lax.axis_size("fcol")
    owners = row_devs * col_devs
    row_here = lax.axis_index("frow")
    col_here = lax.axis_index("fcol")
    width = child_tiles.shape[1]
    held = child_tiles.shape[0]
    slot_count = owners * CAP
    owner_of = tile_target[:, 0]
    block_of = tile_target[:, 1]
    tile_order = jnp.arange(held, dtype=jnp.int32)
    same_owner = owner_of[:, None] == owner_of[None, :]
    earlier = tile_order[None, :] < tile_order[:, None]
    rank_of = jnp.sum(jnp.where(same_owner & earlier, 1, 0), axis=1).astype(jnp.int32)
    slot_of = owner_of * CAP + rank_of
    slot_match = slot_of[None, :] == jnp.arange(slot_count, dtype=jnp.int32)[:, None]
    source_tile = jnp.sum(jnp.where(slot_match, tile_order[None, :], 0), axis=1)
    filled = jnp.any(slot_match, axis=1)
    own_perms = jnp.stack([tile_rows, tile_cols], axis=1)
    placed_here, _ = place_tiles((child_tiles[None], own_perms[None], block_of[None]))
    placed_here = placed_here[0]
    send_tiles = jnp.where(
        filled[:, None, None],
        jnp.take(placed_here, source_tile, axis=0),
        jnp.zeros((), jnp.bfloat16),
    )
    send_blocks = jnp.where(filled, jnp.take(block_of, source_tile, axis=0), -1)
    placed = lax.all_to_all(
        send_tiles.reshape(owners, CAP, width, width),
        ("frow", "fcol"),
        split_axis=0,
        concat_axis=0,
        tiled=True,
    )
    blocks_in = lax.all_to_all(
        send_blocks.reshape(owners, CAP),
        ("frow", "fcol"),
        split_axis=0,
        concat_axis=0,
        tiled=True,
    )
    local = front_orig[0, :, 0, :]
    row_blocks = local.shape[0] // width
    col_blocks = local.shape[1] // width
    block_ids = jnp.arange(row_blocks * col_blocks, dtype=jnp.int32)
    block_onehot = (blocks_in.reshape(1, slot_count) == block_ids[:, None]).astype(jnp.bfloat16)
    summed = jnp.dot(
        block_onehot, placed.reshape(slot_count, width * width), preferred_element_type=jnp.float32
    )
    added = (
        summed.reshape(row_blocks, col_blocks, width, width)
        .transpose(0, 2, 1, 3)
        .reshape(local.shape)
    )
    matrix = local + added
    local_rows = jnp.arange(local.shape[0], dtype=jnp.int32)
    local_cols = jnp.arange(local.shape[1], dtype=jnp.int32)
    global_rows = (local_rows // width * row_devs + row_here) * width + local_rows % width
    global_cols = (local_cols // width * col_devs + col_here) * width + local_cols % width
    total = NPANEL * PW
    hi = lax.Precision.HIGH

    first_row = lax.all_gather(
        matrix[:width, :width].astype(jnp.bfloat16), "fcol", axis=1, tiled=True
    )[:, :total]
    split = total // 2
    left = lax.all_gather(first_row[:, :split], "frow", axis=0, tiled=True)[:total]
    left, right_src = lax.optimization_barrier((left, first_row[:, split:]))
    right = lax.all_gather(right_src, "frow", axis=0, tiled=True)[:total]
    right, own_column = lax.optimization_barrier((right, matrix[:, :width]))
    corner = jnp.concatenate([left, right], axis=1).astype(jnp.float32)
    row_panel = lax.all_gather(
        own_column.astype(jnp.bfloat16), "fcol", axis=1, tiled=True
    )[:, :total]
    half = row_devs // col_devs
    pairs = []
    for src_row in range(row_devs):
        for src_col in range(col_devs):
            dst_row = (src_row // col_devs) * col_devs + src_col
            dst_col = src_row % col_devs
            pairs.append((src_row * col_devs + src_col, dst_row * col_devs + dst_col))
    piece = lax.dynamic_slice_in_dim(row_panel, col_here * width, width, axis=0)
    piece = lax.ppermute(piece, ("frow", "fcol"), pairs)
    col_all = lax.all_gather(piece, "frow", axis=0, tiled=False)
    col_panel = (
        col_all.reshape(half, row_blocks, width, total)
        .transpose(1, 0, 2, 3)
        .reshape(local.shape[1], total)
    )
    rows_all = jnp.concatenate([row_panel, col_panel], axis=0).astype(jnp.float32)
    n_own = local.shape[0]
    factor_full = jnp.zeros((total, total), jnp.float32)
    pieces = []
    eye = jnp.eye(PW, dtype=jnp.float32)
    for panel_idx in range(NPANEL):
        start = panel_idx * PW
        stop = start + PW
        diag_block = corner[start:stop, start:stop]
        symmetric = jnp.tril(diag_block) + jnp.tril(diag_block, -1).T
        factor = jnp.linalg.cholesky(symmetric)
        inverse = lax.linalg.triangular_solve(factor, eye, left_side=True, lower=True)
        factor_full = factor_full.at[start:stop, start:stop].set(factor)
        solved_rows = jnp.dot(
            rows_all[:, start:stop], inverse.T, precision=hi, preferred_element_type=jnp.float32
        )
        pieces.append(solved_rows)
        if stop < total:
            below = jnp.dot(
                corner[stop:, start:stop], inverse.T, precision=hi, preferred_element_type=jnp.float32
            )
            factor_full = factor_full.at[stop:, start:stop].set(below)
            corner = corner.at[stop:, stop:].add(
                -jnp.dot(below, below.T, precision=hi, preferred_element_type=jnp.float32)
            )
            rows_all = rows_all.at[:, stop:].add(
                -jnp.dot(solved_rows, below.T, precision=hi, preferred_element_type=jnp.float32)
            )
    solved = jnp.concatenate(pieces, axis=1)
    row_factor = solved[:n_own]
    col_factor = solved[n_own:]
    matrix = subtract_product(matrix, row_factor, col_factor)
    in_corner = (global_rows < total)[:, None]
    corner_rows = jnp.take(factor_full, jnp.clip(global_rows, 0, total - 1), axis=0)
    panel_vals = jnp.where(in_corner, corner_rows, row_factor)
    own_part = lax.dynamic_slice_in_dim(panel_vals, col_here * width, width, axis=1)
    matrix = matrix.at[:, :width].set(own_part)
    lower_part = global_rows[:, None] >= global_cols[None, :]
    result = jnp.where(lower_part, matrix, 0.0)
    return result[None, :, None, :]


def solution(mesh):
    return jax.shard_map(
        shards,
        mesh=mesh,
        in_specs=(
            P("frow", None, "fcol", None),
            P(("frow", "fcol"), None, None),
            P(("frow", "fcol"), None),
            P(("frow", "fcol"), None),
            P(("frow", "fcol"), None),
        ),
        out_specs=P("frow", None, "fcol", None),
        check_vma=False,
    )
```

```python
import jax
import jax.numpy as jnp
from jax import lax
from jax.sharding import PartitionSpec as P

PW = 512
NPANEL = 2
CAP = 2


def as_sent(x):
    return jax.tree.map(lambda a: a.astype(jnp.bfloat16) if a.dtype == jnp.float32 else a, x)


def broadcast(block, axis, source):
    block = jnp.where(lax.axis_index(axis) == source, block, jnp.zeros_like(block))
    return lax.psum(block, axis)


def place_tiles(received):
    tile_block, perm_block, target_block = received
    width = tile_block.shape[-1]
    positions = jnp.arange(width, dtype=jnp.int32)
    row_onehot = (perm_block[:, :, 0, None, :] == positions[:, None]).astype(jnp.bfloat16)
    col_onehot = (perm_block[:, :, 1, None, :] == positions[:, None]).astype(jnp.bfloat16)
    moved = jnp.einsum(
        "abxi,abij->abxj", row_onehot, tile_block, preferred_element_type=jnp.float32
    ).astype(jnp.bfloat16)
    placed = jnp.einsum(
        "abxj,abyj->abxy", moved, col_onehot, preferred_element_type=jnp.float32
    ).astype(jnp.bfloat16)
    return (placed, target_block)


def subtract_product(matrix, row_factor, col_factor):
    product = jnp.dot(
        row_factor,
        col_factor.T,
        precision=lax.Precision.HIGH,
        preferred_element_type=jnp.float32,
    )
    return matrix - product


def shards(front_orig, child_tiles, tile_target, tile_rows, tile_cols):
    row_devs = lax.axis_size("frow")
    col_devs = lax.axis_size("fcol")
    owners = row_devs * col_devs
    row_here = lax.axis_index("frow")
    col_here = lax.axis_index("fcol")
    width = child_tiles.shape[1]
    held = child_tiles.shape[0]
    slot_count = owners * CAP
    owner_of = tile_target[:, 0]
    block_of = tile_target[:, 1]
    tile_order = jnp.arange(held, dtype=jnp.int32)
    same_owner = owner_of[:, None] == owner_of[None, :]
    earlier = tile_order[None, :] < tile_order[:, None]
    rank_of = jnp.sum(jnp.where(same_owner & earlier, 1, 0), axis=1).astype(jnp.int32)
    slot_of = owner_of * CAP + rank_of
    slot_match = slot_of[None, :] == jnp.arange(slot_count, dtype=jnp.int32)[:, None]
    source_tile = jnp.sum(jnp.where(slot_match, tile_order[None, :], 0), axis=1)
    filled = jnp.any(slot_match, axis=1)
    own_perms = jnp.stack([tile_rows, tile_cols], axis=1)
    placed_here, _ = place_tiles((child_tiles[None], own_perms[None], block_of[None]))
    placed_here = placed_here[0]
    send_tiles = jnp.where(
        filled[:, None, None],
        jnp.take(placed_here, source_tile, axis=0),
        jnp.zeros((), jnp.bfloat16),
    )
    send_blocks = jnp.where(filled, jnp.take(block_of, source_tile, axis=0), -1)
    placed = lax.all_to_all(
        send_tiles.reshape(owners, CAP, width, width),
        ("frow", "fcol"),
        split_axis=0,
        concat_axis=0,
        tiled=True,
    )
    blocks_in = lax.all_to_all(
        send_blocks.reshape(owners, CAP),
        ("frow", "fcol"),
        split_axis=0,
        concat_axis=0,
        tiled=True,
    )
    local = front_orig[0, :, 0, :]
    row_blocks = local.shape[0] // width
    col_blocks = local.shape[1] // width
    block_ids = jnp.arange(row_blocks * col_blocks, dtype=jnp.int32)
    block_onehot = (blocks_in.reshape(1, slot_count) == block_ids[:, None]).astype(jnp.bfloat16)
    summed = jnp.dot(
        block_onehot, placed.reshape(slot_count, width * width), preferred_element_type=jnp.float32
    )
    added = (
        summed.reshape(row_blocks, col_blocks, width, width)
        .transpose(0, 2, 1, 3)
        .reshape(local.shape)
    )
    matrix = local + added
    first_ids = jnp.arange(row_blocks, dtype=jnp.int32) * col_blocks
    first_onehot = (blocks_in.reshape(1, slot_count) == first_ids[:, None]).astype(jnp.bfloat16)
    first_added = jnp.dot(
        first_onehot, placed.reshape(slot_count, width * width), preferred_element_type=jnp.float32
    ).reshape(local.shape[0], width)
    first_column = local[:, :width] + first_added
    local_rows = jnp.arange(local.shape[0], dtype=jnp.int32)
    local_cols = jnp.arange(local.shape[1], dtype=jnp.int32)
    global_rows = (local_rows // width * row_devs + row_here) * width + local_rows % width
    global_cols = (local_cols // width * col_devs + col_here) * width + local_cols % width
    total = NPANEL * PW
    hi = lax.Precision.HIGH

    first_row = lax.all_gather(
        first_column[:width].astype(jnp.bfloat16), "fcol", axis=1, tiled=True
    )[:, :total]
    split = total // 2
    left = lax.all_gather(first_row[:, :split], "frow", axis=0, tiled=True)[:total]
    left, right_src = lax.optimization_barrier((left, first_row[:, split:]))
    right = lax.all_gather(right_src, "frow", axis=0, tiled=True)[:total]
    right, own_column = lax.optimization_barrier((right, first_column))
    corner = jnp.concatenate([left, right], axis=1).astype(jnp.float32)
    row_panel = lax.all_gather(
        own_column.astype(jnp.bfloat16), "fcol", axis=1, tiled=True
    )[:, :total]
    half = row_devs // col_devs
    pairs = []
    for src_row in range(row_devs):
        for src_col in range(col_devs):
            dst_row = (src_row // col_devs) * col_devs + src_col
            dst_col = src_row % col_devs
            pairs.append((src_row * col_devs + src_col, dst_row * col_devs + dst_col))
    piece = lax.dynamic_slice_in_dim(row_panel, col_here * width, width, axis=0)
    piece = lax.ppermute(piece, ("frow", "fcol"), pairs)
    col_all = lax.all_gather(piece, "frow", axis=0, tiled=False)
    col_panel = (
        col_all.reshape(half, row_blocks, width, total)
        .transpose(1, 0, 2, 3)
        .reshape(local.shape[1], total)
    )
    rows_all = jnp.concatenate([row_panel, col_panel], axis=0).astype(jnp.float32)
    n_own = local.shape[0]
    factor_full = jnp.zeros((total, total), jnp.float32)
    pieces = []
    eye = jnp.eye(PW, dtype=jnp.float32)
    for panel_idx in range(NPANEL):
        start = panel_idx * PW
        stop = start + PW
        diag_block = corner[start:stop, start:stop]
        symmetric = jnp.tril(diag_block) + jnp.tril(diag_block, -1).T
        factor = jnp.linalg.cholesky(symmetric)
        inverse = lax.linalg.triangular_solve(factor, eye, left_side=True, lower=True)
        factor_full = factor_full.at[start:stop, start:stop].set(factor)
        solved_rows = jnp.dot(
            rows_all[:, start:stop], inverse.T, precision=hi, preferred_element_type=jnp.float32
        )
        pieces.append(solved_rows)
        if stop < total:
            below = jnp.dot(
                corner[stop:, start:stop], inverse.T, precision=hi, preferred_element_type=jnp.float32
            )
            factor_full = factor_full.at[stop:, start:stop].set(below)
            corner = corner.at[stop:, stop:].add(
                -jnp.dot(below, below.T, precision=hi, preferred_element_type=jnp.float32)
            )
            rows_all = rows_all.at[:, stop:].add(
                -jnp.dot(solved_rows, below.T, precision=hi, preferred_element_type=jnp.float32)
            )
    solved = jnp.concatenate(pieces, axis=1)
    row_factor = solved[:n_own]
    col_factor = solved[n_own:]
    matrix = subtract_product(matrix, row_factor, col_factor)
    in_corner = (global_rows < total)[:, None]
    corner_rows = jnp.take(factor_full, jnp.clip(global_rows, 0, total - 1), axis=0)
    panel_vals = jnp.where(in_corner, corner_rows, row_factor)
    own_part = lax.dynamic_slice_in_dim(panel_vals, col_here * width, width, axis=1)
    matrix = matrix.at[:, :width].set(own_part)
    lower_part = global_rows[:, None] >= global_cols[None, :]
    result = jnp.where(lower_part, matrix, 0.0)
    return result[None, :, None, :]


def solution(mesh):
    return jax.shard_map(
        shards,
        mesh=mesh,
        in_specs=(
            P("frow", None, "fcol", None),
            P(("frow", "fcol"), None, None),
            P(("frow", "fcol"), None),
            P(("frow", "fcol"), None),
            P(("frow", "fcol"), None),
        ),
        out_specs=P("frow", None, "fcol", None),
        check_vma=False,
    )
```

```python
import jax
import jax.numpy as jnp
from jax import lax
from jax.sharding import PartitionSpec as P

PW = 512
NPANEL = 2
CAP = 2


def as_sent(x):
    return jax.tree.map(lambda a: a.astype(jnp.bfloat16) if a.dtype == jnp.float32 else a, x)


def broadcast(block, axis, source):
    block = jnp.where(lax.axis_index(axis) == source, block, jnp.zeros_like(block))
    return lax.psum(block, axis)


def place_tiles(received):
    tile_block, perm_block, target_block = received
    width = tile_block.shape[-1]
    positions = jnp.arange(width, dtype=jnp.int32)
    row_onehot = (perm_block[:, :, 0, None, :] == positions[:, None]).astype(jnp.bfloat16)
    col_onehot = (perm_block[:, :, 1, None, :] == positions[:, None]).astype(jnp.bfloat16)
    moved = jnp.einsum(
        "abxi,abij->abxj", row_onehot, tile_block, preferred_element_type=jnp.float32
    ).astype(jnp.bfloat16)
    placed = jnp.einsum(
        "abxj,abyj->abxy", moved, col_onehot, preferred_element_type=jnp.float32
    ).astype(jnp.bfloat16)
    return (placed, target_block)


def subtract_product(matrix, row_factor, col_factor):
    product = jnp.dot(
        row_factor,
        col_factor.T,
        precision=lax.Precision.HIGH,
        preferred_element_type=jnp.float32,
    )
    return matrix - product


def shards(front_orig, child_tiles, tile_target, tile_rows, tile_cols):
    row_devs = lax.axis_size("frow")
    col_devs = lax.axis_size("fcol")
    owners = row_devs * col_devs
    row_here = lax.axis_index("frow")
    col_here = lax.axis_index("fcol")
    width = child_tiles.shape[1]
    held = child_tiles.shape[0]
    slot_count = owners * CAP
    owner_of = tile_target[:, 0]
    block_of = tile_target[:, 1]
    tile_order = jnp.arange(held, dtype=jnp.int32)
    same_owner = owner_of[:, None] == owner_of[None, :]
    earlier = tile_order[None, :] < tile_order[:, None]
    rank_of = jnp.sum(jnp.where(same_owner & earlier, 1, 0), axis=1).astype(jnp.int32)
    slot_of = owner_of * CAP + rank_of
    slot_match = slot_of[None, :] == jnp.arange(slot_count, dtype=jnp.int32)[:, None]
    source_tile = jnp.sum(jnp.where(slot_match, tile_order[None, :], 0), axis=1)
    filled = jnp.any(slot_match, axis=1)
    own_perms = jnp.stack([tile_rows, tile_cols], axis=1)
    placed_here, _ = place_tiles((child_tiles[None], own_perms[None], block_of[None]))
    placed_here = placed_here[0]
    send_tiles = jnp.where(
        filled[:, None, None],
        jnp.take(placed_here, source_tile, axis=0),
        jnp.zeros((), jnp.bfloat16),
    )
    send_blocks = jnp.where(filled, jnp.take(block_of, source_tile, axis=0), -1)
    placed = lax.all_to_all(
        send_tiles.reshape(owners, CAP, width, width),
        ("frow", "fcol"),
        split_axis=0,
        concat_axis=0,
        tiled=True,
    )
    blocks_in = lax.all_to_all(
        send_blocks.reshape(owners, CAP),
        ("frow", "fcol"),
        split_axis=0,
        concat_axis=0,
        tiled=True,
    )
    local = front_orig[0, :, 0, :]
    row_blocks = local.shape[0] // width
    col_blocks = local.shape[1] // width
    block_ids = jnp.arange(row_blocks * col_blocks, dtype=jnp.int32)
    block_onehot = (blocks_in.reshape(1, slot_count) == block_ids[:, None]).astype(jnp.bfloat16)
    summed = jnp.dot(
        block_onehot, placed.reshape(slot_count, width * width), preferred_element_type=jnp.float32
    )
    added = (
        summed.reshape(row_blocks, col_blocks, width, width)
        .transpose(0, 2, 1, 3)
        .reshape(local.shape)
    )
    matrix = local + added
    first_ids = jnp.arange(row_blocks, dtype=jnp.int32) * col_blocks
    first_onehot = (blocks_in.reshape(1, slot_count) == first_ids[:, None]).astype(jnp.bfloat16)
    first_added = jnp.dot(
        first_onehot, placed.reshape(slot_count, width * width), preferred_element_type=jnp.float32
    ).reshape(local.shape[0], width)
    first_column = local[:, :width] + first_added
    local_rows = jnp.arange(local.shape[0], dtype=jnp.int32)
    local_cols = jnp.arange(local.shape[1], dtype=jnp.int32)
    global_rows = (local_rows // width * row_devs + row_here) * width + local_rows % width
    global_cols = (local_cols // width * col_devs + col_here) * width + local_cols % width
    total = NPANEL * PW
    hi = lax.Precision.HIGH

    first_row = lax.all_gather(
        first_column[:width].astype(jnp.bfloat16), "fcol", axis=1, tiled=True
    )[:, :total]
    split = total // 2
    left = lax.all_gather(first_row[:, :split], "frow", axis=0, tiled=True)[:total]
    left, right_src = lax.optimization_barrier((left, first_row[:, split:]))
    right = lax.all_gather(right_src, "frow", axis=0, tiled=True)[:total]
    right, own_column = lax.optimization_barrier((right, first_column))
    corner = jnp.concatenate([left, right], axis=1).astype(jnp.float32)
    row_panel = lax.all_gather(
        own_column.astype(jnp.bfloat16), "fcol", axis=1, tiled=True
    )[:, :total]
    half = row_devs // col_devs
    pairs = []
    for src_row in range(row_devs):
        for src_col in range(col_devs):
            dst_row = (src_row // col_devs) * col_devs + src_col
            dst_col = src_row % col_devs
            pairs.append((src_row * col_devs + src_col, dst_row * col_devs + dst_col))
    piece = lax.dynamic_slice_in_dim(row_panel, col_here * width, width, axis=0)
    piece = lax.ppermute(piece, ("frow", "fcol"), pairs)
    col_all = lax.all_gather(piece, "frow", axis=0, tiled=False)
    col_panel = (
        col_all.reshape(half, row_blocks, width, total)
        .transpose(1, 0, 2, 3)
        .reshape(local.shape[1], total)
    )
    rows_all = jnp.concatenate([row_panel, col_panel], axis=0).astype(jnp.float32)
    n_own = local.shape[0]
    full = lax.Precision.HIGHEST
    corner_blocks = total // width
    factor_full = jnp.zeros((total, total), jnp.float32)
    eye = jnp.eye(width, dtype=jnp.float32)
    inverses = []
    for blk in range(corner_blocks):
        start = blk * width
        stop = start + width
        diag_block = corner[start:stop, start:stop]
        symmetric = jnp.tril(diag_block) + jnp.tril(diag_block, -1).T
        factor = jnp.linalg.cholesky(symmetric)
        inverse = lax.linalg.triangular_solve(factor, eye, left_side=True, lower=True)
        inverses.append(inverse)
        factor_full = factor_full.at[start:stop, start:stop].set(factor)
        if stop < total:
            below = jnp.dot(
                corner[stop:, start:stop], inverse.T, precision=full, preferred_element_type=jnp.float32
            )
            factor_full = factor_full.at[stop:, start:stop].set(below)
            corner = corner.at[stop:, stop:].add(
                -jnp.dot(below, below.T, precision=full, preferred_element_type=jnp.float32)
            )
    inv_blocks = jnp.stack(inverses)
    size = width
    while size < total:
        pairs_n = total // (2 * size)
        grid = factor_full.reshape(pairs_n, 2 * size, pairs_n, 2 * size)
        idx = jnp.arange(pairs_n)
        diag_pairs = grid[idx, :, idx, :]
        lower_left = diag_pairs[:, size:, :size]
        upper_inv = inv_blocks[0::2]
        lower_inv = inv_blocks[1::2]
        mixed = -jnp.einsum(
            "nab,nbc->nac",
            lower_inv,
            jnp.einsum("nab,nbc->nac", lower_left, upper_inv, precision=full),
            precision=full,
        )
        zeros = jnp.zeros_like(mixed)
        top = jnp.concatenate([upper_inv, zeros], axis=2)
        bottom = jnp.concatenate([mixed, lower_inv], axis=2)
        inv_blocks = jnp.concatenate([top, bottom], axis=1)
        size *= 2
    factor_inverse = inv_blocks[0]
    solved = jnp.dot(rows_all, factor_inverse.T, precision=hi, preferred_element_type=jnp.float32)
    row_factor = solved[:n_own]
    col_factor = solved[n_own:]
    matrix = subtract_product(matrix, row_factor, col_factor)
    in_corner = (global_rows < total)[:, None]
    corner_rows = jnp.take(factor_full, jnp.clip(global_rows, 0, total - 1), axis=0)
    panel_vals = jnp.where(in_corner, corner_rows, row_factor)
    own_part = lax.dynamic_slice_in_dim(panel_vals, col_here * width, width, axis=1)
    matrix = matrix.at[:, :width].set(own_part)
    lower_part = global_rows[:, None] >= global_cols[None, :]
    result = jnp.where(lower_part, matrix, 0.0)
    return result[None, :, None, :]


def solution(mesh):
    return jax.shard_map(
        shards,
        mesh=mesh,
        in_specs=(
            P("frow", None, "fcol", None),
            P(("frow", "fcol"), None, None),
            P(("frow", "fcol"), None),
            P(("frow", "fcol"), None),
            P(("frow", "fcol"), None),
        ),
        out_specs=P("frow", None, "fcol", None),
        check_vma=False,
    )
```

```python
import jax
import jax.numpy as jnp
from jax import lax
from jax.sharding import PartitionSpec as P

PW = 512
NPANEL = 2
CAP = 2


def as_sent(x):
    return jax.tree.map(lambda a: a.astype(jnp.bfloat16) if a.dtype == jnp.float32 else a, x)


def broadcast(block, axis, source):
    block = jnp.where(lax.axis_index(axis) == source, block, jnp.zeros_like(block))
    return lax.psum(block, axis)


def place_tiles(received):
    tile_block, perm_block, target_block = received
    width = tile_block.shape[-1]
    positions = jnp.arange(width, dtype=jnp.int32)
    row_onehot = (perm_block[:, :, 0, None, :] == positions[:, None]).astype(jnp.bfloat16)
    col_onehot = (perm_block[:, :, 1, None, :] == positions[:, None]).astype(jnp.bfloat16)
    moved = jnp.einsum(
        "abxi,abij->abxj", row_onehot, tile_block, preferred_element_type=jnp.float32
    ).astype(jnp.bfloat16)
    placed = jnp.einsum(
        "abxj,abyj->abxy", moved, col_onehot, preferred_element_type=jnp.float32
    ).astype(jnp.bfloat16)
    return (placed, target_block)


def subtract_product(matrix, row_factor, col_factor):
    product = jnp.dot(
        row_factor,
        col_factor.T,
        precision=lax.Precision.HIGH,
        preferred_element_type=jnp.float32,
    )
    return matrix - product


def shards(front_orig, child_tiles, tile_target, tile_rows, tile_cols):
    row_devs = lax.axis_size("frow")
    col_devs = lax.axis_size("fcol")
    owners = row_devs * col_devs
    row_here = lax.axis_index("frow")
    col_here = lax.axis_index("fcol")
    width = child_tiles.shape[1]
    held = child_tiles.shape[0]
    slot_count = owners * CAP
    owner_of = tile_target[:, 0]
    block_of = tile_target[:, 1]
    tile_order = jnp.arange(held, dtype=jnp.int32)
    same_owner = owner_of[:, None] == owner_of[None, :]
    earlier = tile_order[None, :] < tile_order[:, None]
    rank_of = jnp.sum(jnp.where(same_owner & earlier, 1, 0), axis=1).astype(jnp.int32)
    slot_of = owner_of * CAP + rank_of
    slot_match = slot_of[None, :] == jnp.arange(slot_count, dtype=jnp.int32)[:, None]
    source_tile = jnp.sum(jnp.where(slot_match, tile_order[None, :], 0), axis=1)
    filled = jnp.any(slot_match, axis=1)
    own_perms = jnp.stack([tile_rows, tile_cols], axis=1)
    placed_here, _ = place_tiles((child_tiles[None], own_perms[None], block_of[None]))
    placed_here = placed_here[0]
    send_tiles = jnp.where(
        filled[:, None, None],
        jnp.take(placed_here, source_tile, axis=0),
        jnp.zeros((), jnp.bfloat16),
    )
    send_blocks = jnp.where(filled, jnp.take(block_of, source_tile, axis=0), -1)
    placed = lax.all_to_all(
        send_tiles.reshape(owners, CAP, width, width),
        ("frow", "fcol"),
        split_axis=0,
        concat_axis=0,
        tiled=True,
    )
    blocks_in = lax.all_to_all(
        send_blocks.reshape(owners, CAP),
        ("frow", "fcol"),
        split_axis=0,
        concat_axis=0,
        tiled=True,
    )
    local = front_orig[0, :, 0, :]
    row_blocks = local.shape[0] // width
    col_blocks = local.shape[1] // width
    block_ids = jnp.arange(row_blocks * col_blocks, dtype=jnp.int32)
    block_onehot = (blocks_in.reshape(1, slot_count) == block_ids[:, None]).astype(jnp.bfloat16)
    summed = jnp.dot(
        block_onehot, placed.reshape(slot_count, width * width), preferred_element_type=jnp.float32
    )
    added = (
        summed.reshape(row_blocks, col_blocks, width, width)
        .transpose(0, 2, 1, 3)
        .reshape(local.shape)
    )
    matrix = local + added
    first_ids = jnp.arange(row_blocks, dtype=jnp.int32) * col_blocks
    first_onehot = (blocks_in.reshape(1, slot_count) == first_ids[:, None]).astype(jnp.bfloat16)
    first_added = jnp.dot(
        first_onehot, placed.reshape(slot_count, width * width), preferred_element_type=jnp.float32
    ).reshape(local.shape[0], width)
    first_column = local[:, :width] + first_added
    local_rows = jnp.arange(local.shape[0], dtype=jnp.int32)
    local_cols = jnp.arange(local.shape[1], dtype=jnp.int32)
    global_rows = (local_rows // width * row_devs + row_here) * width + local_rows % width
    global_cols = (local_cols // width * col_devs + col_here) * width + local_cols % width
    total = NPANEL * PW
    hi = lax.Precision.HIGH

    first_row = lax.all_gather(
        first_column[:width].astype(jnp.bfloat16), "fcol", axis=1, tiled=True
    )[:, :total]
    split = total // 2
    left = lax.all_gather(first_row[:, :split], "frow", axis=0, tiled=True)[:total]
    left, right_src = lax.optimization_barrier((left, first_row[:, split:]))
    right = lax.all_gather(right_src, "frow", axis=0, tiled=True)[:total]
    right, own_column = lax.optimization_barrier((right, first_column))
    corner = jnp.concatenate([left, right], axis=1).astype(jnp.float32)
    row_panel = lax.all_gather(
        own_column.astype(jnp.bfloat16), "fcol", axis=1, tiled=True
    )[:, :total]
    half = row_devs // col_devs
    pairs = []
    for src_row in range(row_devs):
        for src_col in range(col_devs):
            dst_row = (src_row // col_devs) * col_devs + src_col
            dst_col = src_row % col_devs
            pairs.append((src_row * col_devs + src_col, dst_row * col_devs + dst_col))
    piece = lax.dynamic_slice_in_dim(row_panel, col_here * width, width, axis=0)
    piece = lax.ppermute(piece, ("frow", "fcol"), pairs)
    col_all = lax.all_gather(piece, "frow", axis=0, tiled=False)
    col_panel = (
        col_all.reshape(half, row_blocks, width, total)
        .transpose(1, 0, 2, 3)
        .reshape(local.shape[1], total)
    )
    rows_all = jnp.concatenate([row_panel, col_panel], axis=0).astype(jnp.float32)
    n_own = local.shape[0]
    full = lax.Precision.HIGHEST
    corner_blocks = total // width
    factor_full = jnp.zeros((total, total), jnp.float32)
    eye = jnp.eye(width, dtype=jnp.float32)
    inverses = []
    for blk in range(corner_blocks):
        start = blk * width
        stop = start + width
        diag_block = corner[start:stop, start:stop]
        symmetric = jnp.tril(diag_block) + jnp.tril(diag_block, -1).T
        factor = jnp.linalg.cholesky(symmetric)
        inverse = lax.linalg.triangular_solve(factor, eye, left_side=True, lower=True)
        inverses.append(inverse)
        factor_full = factor_full.at[start:stop, start:stop].set(factor)
        if stop < total:
            below = jnp.dot(
                corner[stop:, start:stop], inverse.T, precision=full, preferred_element_type=jnp.float32
            )
            factor_full = factor_full.at[stop:, start:stop].set(below)
            corner = corner.at[stop:, stop:].add(
                -jnp.dot(below, below.T, precision=full, preferred_element_type=jnp.float32)
            )
    inv_blocks = jnp.stack(inverses)
    size = width
    while size < total:
        pairs_n = total // (2 * size)
        lower_left = jnp.stack(
            [
                factor_full[(2 * k + 1) * size : (2 * k + 2) * size, 2 * k * size : (2 * k + 1) * size]
                for k in range(pairs_n)
            ]
        )
        upper_inv = inv_blocks[0::2]
        lower_inv = inv_blocks[1::2]
        mixed = -jnp.einsum(
            "nab,nbc->nac",
            lower_inv,
            jnp.einsum("nab,nbc->nac", lower_left, upper_inv, precision=full),
            precision=full,
        )
        zeros = jnp.zeros_like(mixed)
        top = jnp.concatenate([upper_inv, zeros], axis=2)
        bottom = jnp.concatenate([mixed, lower_inv], axis=2)
        inv_blocks = jnp.concatenate([top, bottom], axis=1)
        size *= 2
    factor_inverse = inv_blocks[0]
    solved = jnp.dot(rows_all, factor_inverse.T, precision=hi, preferred_element_type=jnp.float32)
    row_factor = solved[:n_own]
    col_factor = solved[n_own:]
    matrix = subtract_product(matrix, row_factor, col_factor)
    corner_rows = lax.dynamic_slice_in_dim(
        factor_full, jnp.minimum(row_here, total // width - 1) * width, width, axis=0
    )
    head = jnp.where(row_here * width < total, corner_rows, row_factor[:width])
    panel_vals = jnp.concatenate([head, row_factor[width:]], axis=0)
    own_part = lax.dynamic_slice_in_dim(panel_vals, col_here * width, width, axis=1)
    matrix = matrix.at[:, :width].set(own_part)
    lower_part = global_rows[:, None] >= global_cols[None, :]
    result = jnp.where(lower_part, matrix, 0.0)
    return result[None, :, None, :]


def solution(mesh):
    return jax.shard_map(
        shards,
        mesh=mesh,
        in_specs=(
            P("frow", None, "fcol", None),
            P(("frow", "fcol"), None, None),
            P(("frow", "fcol"), None),
            P(("frow", "fcol"), None),
            P(("frow", "fcol"), None),
        ),
        out_specs=P("frow", None, "fcol", None),
        check_vma=False,
    )
```

```python
import jax
import jax.numpy as jnp
from jax import lax
from jax.sharding import PartitionSpec as P

PW = 512
NPANEL = 2
CAP = 2


def as_sent(x):
    return jax.tree.map(lambda a: a.astype(jnp.bfloat16) if a.dtype == jnp.float32 else a, x)


def broadcast(block, axis, source):
    block = jnp.where(lax.axis_index(axis) == source, block, jnp.zeros_like(block))
    return lax.psum(block, axis)


def place_tiles(received):
    tile_block, perm_block, target_block = received
    width = tile_block.shape[-1]
    positions = jnp.arange(width, dtype=jnp.int32)
    row_onehot = (perm_block[:, :, 0, None, :] == positions[:, None]).astype(jnp.bfloat16)
    col_onehot = (perm_block[:, :, 1, None, :] == positions[:, None]).astype(jnp.bfloat16)
    moved = jnp.einsum(
        "abxi,abij->abxj", row_onehot, tile_block, preferred_element_type=jnp.float32
    ).astype(jnp.bfloat16)
    placed = jnp.einsum(
        "abxj,abyj->abxy", moved, col_onehot, preferred_element_type=jnp.float32
    ).astype(jnp.bfloat16)
    return (placed, target_block)


def subtract_product(matrix, row_factor, col_factor):
    product = jnp.dot(
        row_factor,
        col_factor.T,
        precision=lax.Precision.HIGH,
        preferred_element_type=jnp.float32,
    )
    return matrix - product


def shards(front_orig, child_tiles, tile_target, tile_rows, tile_cols):
    row_devs = lax.axis_size("frow")
    col_devs = lax.axis_size("fcol")
    owners = row_devs * col_devs
    row_here = lax.axis_index("frow")
    col_here = lax.axis_index("fcol")
    width = child_tiles.shape[1]
    held = child_tiles.shape[0]
    slot_count = owners * CAP
    owner_of = tile_target[:, 0]
    block_of = tile_target[:, 1]
    tile_order = jnp.arange(held, dtype=jnp.int32)
    same_owner = owner_of[:, None] == owner_of[None, :]
    earlier = tile_order[None, :] < tile_order[:, None]
    rank_of = jnp.sum(jnp.where(same_owner & earlier, 1, 0), axis=1).astype(jnp.int32)
    slot_of = owner_of * CAP + rank_of
    slot_match = slot_of[None, :] == jnp.arange(slot_count, dtype=jnp.int32)[:, None]
    source_tile = jnp.sum(jnp.where(slot_match, tile_order[None, :], 0), axis=1)
    filled = jnp.any(slot_match, axis=1)
    own_perms = jnp.stack([tile_rows, tile_cols], axis=1)
    placed_here, _ = place_tiles((child_tiles[None], own_perms[None], block_of[None]))
    placed_here = placed_here[0]
    send_tiles = jnp.where(
        filled[:, None, None],
        jnp.take(placed_here, source_tile, axis=0),
        jnp.zeros((), jnp.bfloat16),
    )
    send_blocks = jnp.where(filled, jnp.take(block_of, source_tile, axis=0), -1)
    placed = lax.all_to_all(
        send_tiles.reshape(owners, CAP, width, width),
        ("frow", "fcol"),
        split_axis=0,
        concat_axis=0,
        tiled=True,
    )
    blocks_in = lax.all_to_all(
        send_blocks.reshape(owners, CAP),
        ("frow", "fcol"),
        split_axis=0,
        concat_axis=0,
        tiled=True,
    )
    local = front_orig[0, :, 0, :]
    row_blocks = local.shape[0] // width
    col_blocks = local.shape[1] // width
    block_ids = jnp.arange(row_blocks * col_blocks, dtype=jnp.int32)
    block_onehot = (blocks_in.reshape(1, slot_count) == block_ids[:, None]).astype(jnp.bfloat16)
    summed = jnp.dot(
        block_onehot, placed.reshape(slot_count, width * width), preferred_element_type=jnp.float32
    )
    added = (
        summed.reshape(row_blocks, col_blocks, width, width)
        .transpose(0, 2, 1, 3)
        .reshape(local.shape)
    )
    matrix = local + added
    first_ids = jnp.arange(row_blocks, dtype=jnp.int32) * col_blocks
    first_onehot = (blocks_in.reshape(1, slot_count) == first_ids[:, None]).astype(jnp.bfloat16)
    first_added = jnp.dot(
        first_onehot, placed.reshape(slot_count, width * width), preferred_element_type=jnp.float32
    ).reshape(local.shape[0], width)
    first_column = local[:, :width] + first_added
    local_rows = jnp.arange(local.shape[0], dtype=jnp.int32)
    local_cols = jnp.arange(local.shape[1], dtype=jnp.int32)
    global_rows = (local_rows // width * row_devs + row_here) * width + local_rows % width
    global_cols = (local_cols // width * col_devs + col_here) * width + local_cols % width
    total = NPANEL * PW
    hi = lax.Precision.HIGH

    first_row = lax.all_gather(
        first_column[:width].astype(jnp.bfloat16), "fcol", axis=1, tiled=True
    )[:, :total]
    split = total // 2
    left = lax.all_gather(first_row[:, :split], "frow", axis=0, tiled=True)[:total]
    left, right_src, matrix = lax.optimization_barrier((left, first_row[:, split:], matrix))
    right = lax.all_gather(right_src, "frow", axis=0, tiled=True)[:total]
    right, own_column = lax.optimization_barrier((right, first_column))
    corner = jnp.concatenate([left, right], axis=1).astype(jnp.float32)
    row_panel = lax.all_gather(
        own_column.astype(jnp.bfloat16), "fcol", axis=1, tiled=True
    )[:, :total]
    half = row_devs // col_devs
    pairs = []
    for src_row in range(row_devs):
        for src_col in range(col_devs):
            dst_row = (src_row // col_devs) * col_devs + src_col
            dst_col = src_row % col_devs
            pairs.append((src_row * col_devs + src_col, dst_row * col_devs + dst_col))
    piece = lax.dynamic_slice_in_dim(row_panel, col_here * width, width, axis=0)
    piece = lax.ppermute(piece, ("frow", "fcol"), pairs)
    col_all = lax.all_gather(piece, "frow", axis=0, tiled=False)
    col_panel = (
        col_all.reshape(half, row_blocks, width, total)
        .transpose(1, 0, 2, 3)
        .reshape(local.shape[1], total)
    )
    rows_all = jnp.concatenate([row_panel, col_panel], axis=0).astype(jnp.float32)
    n_own = local.shape[0]
    full = lax.Precision.HIGHEST
    corner_blocks = total // width
    factor_full = jnp.zeros((total, total), jnp.float32)
    eye = jnp.eye(width, dtype=jnp.float32)
    inverses = []
    for blk in range(corner_blocks):
        start = blk * width
        stop = start + width
        diag_block = corner[start:stop, start:stop]
        symmetric = jnp.tril(diag_block) + jnp.tril(diag_block, -1).T
        factor = jnp.linalg.cholesky(symmetric)
        inverse = lax.linalg.triangular_solve(factor, eye, left_side=True, lower=True)
        inverses.append(inverse)
        factor_full = factor_full.at[start:stop, start:stop].set(factor)
        if stop < total:
            below = jnp.dot(
                corner[stop:, start:stop], inverse.T, precision=full, preferred_element_type=jnp.float32
            )
            factor_full = factor_full.at[stop:, start:stop].set(below)
            corner = corner.at[stop:, stop:].add(
                -jnp.dot(below, below.T, precision=full, preferred_element_type=jnp.float32)
            )
    inv_blocks = jnp.stack(inverses)
    size = width
    while size < total:
        pairs_n = total // (2 * size)
        lower_left = jnp.stack(
            [
                factor_full[(2 * k + 1) * size : (2 * k + 2) * size, 2 * k * size : (2 * k + 1) * size]
                for k in range(pairs_n)
            ]
        )
        upper_inv = inv_blocks[0::2]
        lower_inv = inv_blocks[1::2]
        mixed = -jnp.einsum(
            "nab,nbc->nac",
            lower_inv,
            jnp.einsum("nab,nbc->nac", lower_left, upper_inv, precision=full),
            precision=full,
        )
        zeros = jnp.zeros_like(mixed)
        top = jnp.concatenate([upper_inv, zeros], axis=2)
        bottom = jnp.concatenate([mixed, lower_inv], axis=2)
        inv_blocks = jnp.concatenate([top, bottom], axis=1)
        size *= 2
    factor_inverse = inv_blocks[0]
    solved = jnp.dot(rows_all, factor_inverse.T, precision=hi, preferred_element_type=jnp.float32)
    row_factor = solved[:n_own]
    col_factor = solved[n_own:]
    matrix = subtract_product(matrix, row_factor, col_factor)
    corner_rows = lax.dynamic_slice_in_dim(
        factor_full, jnp.minimum(row_here, total // width - 1) * width, width, axis=0
    )
    head = jnp.where(row_here * width < total, corner_rows, row_factor[:width])
    panel_vals = jnp.concatenate([head, row_factor[width:]], axis=0)
    own_part = lax.dynamic_slice_in_dim(panel_vals, col_here * width, width, axis=1)
    matrix = matrix.at[:, :width].set(own_part)
    lower_part = global_rows[:, None] >= global_cols[None, :]
    result = jnp.where(lower_part, matrix, 0.0)
    return result[None, :, None, :]


def solution(mesh):
    return jax.shard_map(
        shards,
        mesh=mesh,
        in_specs=(
            P("frow", None, "fcol", None),
            P(("frow", "fcol"), None, None),
            P(("frow", "fcol"), None),
            P(("frow", "fcol"), None),
            P(("frow", "fcol"), None),
        ),
        out_specs=P("frow", None, "fcol", None),
        check_vma=False,
    )
```

```python
import jax
import jax.numpy as jnp
from jax import lax
from jax.sharding import PartitionSpec as P

PW = 512
NPANEL = 2
CAP = 2


def as_sent(x):
    return jax.tree.map(lambda a: a.astype(jnp.bfloat16) if a.dtype == jnp.float32 else a, x)


def broadcast(block, axis, source):
    block = jnp.where(lax.axis_index(axis) == source, block, jnp.zeros_like(block))
    return lax.psum(block, axis)


def place_tiles(received):
    tile_block, perm_block, target_block = received
    width = tile_block.shape[-1]
    positions = jnp.arange(width, dtype=jnp.int32)
    row_onehot = (perm_block[:, :, 0, None, :] == positions[:, None]).astype(jnp.bfloat16)
    col_onehot = (perm_block[:, :, 1, None, :] == positions[:, None]).astype(jnp.bfloat16)
    moved = jnp.einsum(
        "abxi,abij->abxj", row_onehot, tile_block, preferred_element_type=jnp.float32
    ).astype(jnp.bfloat16)
    placed = jnp.einsum(
        "abxj,abyj->abxy", moved, col_onehot, preferred_element_type=jnp.float32
    ).astype(jnp.bfloat16)
    return (placed, target_block)


def subtract_product(matrix, row_factor, col_factor):
    product = jnp.dot(
        row_factor,
        col_factor.T,
        precision=lax.Precision.HIGH,
        preferred_element_type=jnp.float32,
    )
    return matrix - product


def shards(front_orig, child_tiles, tile_target, tile_rows, tile_cols):
    row_devs = lax.axis_size("frow")
    col_devs = lax.axis_size("fcol")
    owners = row_devs * col_devs
    row_here = lax.axis_index("frow")
    col_here = lax.axis_index("fcol")
    width = child_tiles.shape[1]
    held = child_tiles.shape[0]
    slot_count = owners * CAP
    owner_of = tile_target[:, 0]
    block_of = tile_target[:, 1]
    tile_order = jnp.arange(held, dtype=jnp.int32)
    same_owner = owner_of[:, None] == owner_of[None, :]
    earlier = tile_order[None, :] < tile_order[:, None]
    rank_of = jnp.sum(jnp.where(same_owner & earlier, 1, 0), axis=1).astype(jnp.int32)
    slot_of = owner_of * CAP + rank_of
    slot_match = slot_of[None, :] == jnp.arange(slot_count, dtype=jnp.int32)[:, None]
    source_tile = jnp.sum(jnp.where(slot_match, tile_order[None, :], 0), axis=1)
    filled = jnp.any(slot_match, axis=1)
    own_perms = jnp.stack([tile_rows, tile_cols], axis=1)
    placed_here, _ = place_tiles((child_tiles[None], own_perms[None], block_of[None]))
    placed_here = placed_here[0]
    send_tiles = jnp.where(
        filled[:, None, None],
        jnp.take(placed_here, source_tile, axis=0),
        jnp.zeros((), jnp.bfloat16),
    )
    send_blocks = jnp.where(filled, jnp.take(block_of, source_tile, axis=0), -1)
    placed = lax.all_to_all(
        send_tiles.reshape(owners, CAP, width, width),
        ("frow", "fcol"),
        split_axis=0,
        concat_axis=0,
        tiled=True,
    )
    blocks_in = lax.all_to_all(
        send_blocks.reshape(owners, CAP),
        ("frow", "fcol"),
        split_axis=0,
        concat_axis=0,
        tiled=True,
    )
    local = front_orig[0, :, 0, :]
    row_blocks = local.shape[0] // width
    col_blocks = local.shape[1] // width
    block_ids = jnp.arange(row_blocks * col_blocks, dtype=jnp.int32)
    block_onehot = (blocks_in.reshape(1, slot_count) == block_ids[:, None]).astype(jnp.bfloat16)
    summed = jnp.dot(
        block_onehot, placed.reshape(slot_count, width * width), preferred_element_type=jnp.float32
    )
    added = (
        summed.reshape(row_blocks, col_blocks, width, width)
        .transpose(0, 2, 1, 3)
        .reshape(local.shape)
    )
    matrix = local + added
    first_ids = jnp.arange(row_blocks, dtype=jnp.int32) * col_blocks
    first_onehot = (blocks_in.reshape(1, slot_count) == first_ids[:, None]).astype(jnp.bfloat16)
    first_added = jnp.dot(
        first_onehot, placed.reshape(slot_count, width * width), preferred_element_type=jnp.float32
    ).reshape(local.shape[0], width)
    first_column = local[:, :width] + first_added
    local_rows = jnp.arange(local.shape[0], dtype=jnp.int32)
    local_cols = jnp.arange(local.shape[1], dtype=jnp.int32)
    global_rows = (local_rows // width * row_devs + row_here) * width + local_rows % width
    global_cols = (local_cols // width * col_devs + col_here) * width + local_cols % width
    total = NPANEL * PW
    hi = lax.Precision.HIGH

    first_row = lax.all_gather(
        first_column[:width].astype(jnp.bfloat16), "fcol", axis=1, tiled=True
    )[:, :total]
    split = total // 2
    left = lax.all_gather(first_row[:, :split], "frow", axis=0, tiled=True)[:total]
    left, right_src, matrix = lax.optimization_barrier((left, first_row[:, split:], matrix))
    right = lax.all_gather(right_src, "frow", axis=0, tiled=True)[:total]
    right, own_column = lax.optimization_barrier((right, first_column))
    halves = [left.astype(jnp.float32), right.astype(jnp.float32)]
    row_panel = lax.all_gather(
        own_column.astype(jnp.bfloat16), "fcol", axis=1, tiled=True
    )[:, :total]
    half = row_devs // col_devs
    pairs = []
    for src_row in range(row_devs):
        for src_col in range(col_devs):
            dst_row = (src_row // col_devs) * col_devs + src_col
            dst_col = src_row % col_devs
            pairs.append((src_row * col_devs + src_col, dst_row * col_devs + dst_col))
    piece = lax.dynamic_slice_in_dim(row_panel, col_here * width, width, axis=0)
    piece = lax.ppermute(piece, ("frow", "fcol"), pairs)
    col_all = lax.all_gather(piece, "frow", axis=0, tiled=False)
    col_panel = (
        col_all.reshape(half, row_blocks, width, total)
        .transpose(1, 0, 2, 3)
        .reshape(local.shape[1], total)
    )
    rows_all = jnp.concatenate([row_panel, col_panel], axis=0).astype(jnp.float32)
    n_own = local.shape[0]
    full = lax.Precision.HIGHEST
    corner_blocks = total // width
    factor_full = jnp.zeros((total, total), jnp.float32)
    eye = jnp.eye(width, dtype=jnp.float32)
    inverses = []
    for h, cur in enumerate(halves):
        if h > 0:
            done_cols = factor_full[:, : h * split]
            cur = cur - jnp.dot(
                done_cols,
                done_cols[h * split : (h + 1) * split].T,
                precision=full,
                preferred_element_type=jnp.float32,
            )
        for b in range(split // width):
            start = h * split + b * width
            stop = start + width
            lb = b * width
            diag_block = cur[start:stop, lb : lb + width]
            symmetric = jnp.tril(diag_block) + jnp.tril(diag_block, -1).T
            factor = jnp.linalg.cholesky(symmetric)
            inverse = lax.linalg.triangular_solve(factor, eye, left_side=True, lower=True)
            inverses.append(inverse)
            factor_full = factor_full.at[start:stop, start:stop].set(factor)
            if stop < total:
                below = jnp.dot(
                    cur[stop:, lb : lb + width], inverse.T, precision=full, preferred_element_type=jnp.float32
                )
                factor_full = factor_full.at[stop:, start:stop].set(below)
                if lb + width < split:
                    cur = cur.at[stop:, lb + width :].add(
                        -jnp.dot(
                            below,
                            below[: split - lb - width].T,
                            precision=full,
                            preferred_element_type=jnp.float32,
                        )
                    )
    inv_blocks = jnp.stack(inverses)
    size = width
    while size < total:
        pairs_n = total // (2 * size)
        lower_left = jnp.stack(
            [
                factor_full[(2 * k + 1) * size : (2 * k + 2) * size, 2 * k * size : (2 * k + 1) * size]
                for k in range(pairs_n)
            ]
        )
        upper_inv = inv_blocks[0::2]
        lower_inv = inv_blocks[1::2]
        mixed = -jnp.einsum(
            "nab,nbc->nac",
            lower_inv,
            jnp.einsum("nab,nbc->nac", lower_left, upper_inv, precision=full),
            precision=full,
        )
        zeros = jnp.zeros_like(mixed)
        top = jnp.concatenate([upper_inv, zeros], axis=2)
        bottom = jnp.concatenate([mixed, lower_inv], axis=2)
        inv_blocks = jnp.concatenate([top, bottom], axis=1)
        size *= 2
    factor_inverse = inv_blocks[0]
    solved = jnp.dot(rows_all, factor_inverse.T, precision=hi, preferred_element_type=jnp.float32)
    row_factor = solved[:n_own]
    col_factor = solved[n_own:]
    matrix = subtract_product(matrix, row_factor, col_factor)
    corner_rows = lax.dynamic_slice_in_dim(
        factor_full, jnp.minimum(row_here, total // width - 1) * width, width, axis=0
    )
    head = jnp.where(row_here * width < total, corner_rows, row_factor[:width])
    panel_vals = jnp.concatenate([head, row_factor[width:]], axis=0)
    own_part = lax.dynamic_slice_in_dim(panel_vals, col_here * width, width, axis=1)
    matrix = matrix.at[:, :width].set(own_part)
    lower_part = global_rows[:, None] >= global_cols[None, :]
    result = jnp.where(lower_part, matrix, 0.0)
    return result[None, :, None, :]


def solution(mesh):
    return jax.shard_map(
        shards,
        mesh=mesh,
        in_specs=(
            P("frow", None, "fcol", None),
            P(("frow", "fcol"), None, None),
            P(("frow", "fcol"), None),
            P(("frow", "fcol"), None),
            P(("frow", "fcol"), None),
        ),
        out_specs=P("frow", None, "fcol", None),
        check_vma=False,
    )
```

```python
import jax
import jax.numpy as jnp
from jax import lax
from jax.sharding import PartitionSpec as P

PW = 512
NPANEL = 2
CAP = 2


def as_sent(x):
    return jax.tree.map(lambda a: a.astype(jnp.bfloat16) if a.dtype == jnp.float32 else a, x)


def broadcast(block, axis, source):
    block = jnp.where(lax.axis_index(axis) == source, block, jnp.zeros_like(block))
    return lax.psum(block, axis)


def place_tiles(received):
    tile_block, perm_block, target_block = received
    width = tile_block.shape[-1]
    positions = jnp.arange(width, dtype=jnp.int32)
    row_onehot = (perm_block[:, :, 0, None, :] == positions[:, None]).astype(jnp.bfloat16)
    col_onehot = (perm_block[:, :, 1, None, :] == positions[:, None]).astype(jnp.bfloat16)
    moved = jnp.einsum(
        "abxi,abij->abxj", row_onehot, tile_block, preferred_element_type=jnp.float32
    ).astype(jnp.bfloat16)
    placed = jnp.einsum(
        "abxj,abyj->abxy", moved, col_onehot, preferred_element_type=jnp.float32
    ).astype(jnp.bfloat16)
    return (placed, target_block)


def subtract_product(matrix, row_factor, col_factor):
    product = jnp.dot(
        row_factor,
        col_factor.T,
        precision=lax.Precision.HIGH,
        preferred_element_type=jnp.float32,
    )
    return matrix - product


def shards(front_orig, child_tiles, tile_target, tile_rows, tile_cols):
    row_devs = lax.axis_size("frow")
    col_devs = lax.axis_size("fcol")
    owners = row_devs * col_devs
    row_here = lax.axis_index("frow")
    col_here = lax.axis_index("fcol")
    width = child_tiles.shape[1]
    held = child_tiles.shape[0]
    slot_count = owners * CAP
    owner_of = tile_target[:, 0]
    block_of = tile_target[:, 1]
    tile_order = jnp.arange(held, dtype=jnp.int32)
    same_owner = owner_of[:, None] == owner_of[None, :]
    earlier = tile_order[None, :] < tile_order[:, None]
    rank_of = jnp.sum(jnp.where(same_owner & earlier, 1, 0), axis=1).astype(jnp.int32)
    slot_of = owner_of * CAP + rank_of
    slot_match = slot_of[None, :] == jnp.arange(slot_count, dtype=jnp.int32)[:, None]
    source_tile = jnp.sum(jnp.where(slot_match, tile_order[None, :], 0), axis=1)
    filled = jnp.any(slot_match, axis=1)
    own_perms = jnp.stack([tile_rows, tile_cols], axis=1)
    placed_here, _ = place_tiles((child_tiles[None], own_perms[None], block_of[None]))
    placed_here = placed_here[0]
    send_tiles = jnp.where(
        filled[:, None, None],
        jnp.take(placed_here, source_tile, axis=0),
        jnp.zeros((), jnp.bfloat16),
    )
    placed = lax.all_to_all(
        send_tiles.reshape(owners, CAP, width, width),
        ("frow", "fcol"),
        split_axis=0,
        concat_axis=0,
        tiled=True,
    )
    targets_all = lax.all_gather(tile_target, ("frow", "fcol"), axis=0, tiled=True)
    me = row_here * col_devs + col_here
    mine_all = targets_all[:, 0].reshape(owners, held) == me
    rank_all = jnp.cumsum(mine_all.astype(jnp.int32), axis=1) - 1
    block_all = targets_all[:, 1].reshape(owners, held)
    slot_rank = jnp.arange(CAP, dtype=jnp.int32)
    hit = mine_all[:, None, :] & (rank_all[:, None, :] == slot_rank[None, :, None])
    blocks_in = jnp.where(
        jnp.any(hit, axis=2), jnp.sum(jnp.where(hit, block_all[:, None, :], 0), axis=2), -1
    )
    local = front_orig[0, :, 0, :]
    row_blocks = local.shape[0] // width
    col_blocks = local.shape[1] // width
    block_ids = jnp.arange(row_blocks * col_blocks, dtype=jnp.int32)
    block_onehot = (blocks_in.reshape(1, slot_count) == block_ids[:, None]).astype(jnp.bfloat16)
    summed = jnp.dot(
        block_onehot, placed.reshape(slot_count, width * width), preferred_element_type=jnp.float32
    )
    added = (
        summed.reshape(row_blocks, col_blocks, width, width)
        .transpose(0, 2, 1, 3)
        .reshape(local.shape)
    )
    matrix = local + added
    first_ids = jnp.arange(row_blocks, dtype=jnp.int32) * col_blocks
    first_onehot = (blocks_in.reshape(1, slot_count) == first_ids[:, None]).astype(jnp.bfloat16)
    first_added = jnp.dot(
        first_onehot, placed.reshape(slot_count, width * width), preferred_element_type=jnp.float32
    ).reshape(local.shape[0], width)
    first_column = local[:, :width] + first_added
    local_rows = jnp.arange(local.shape[0], dtype=jnp.int32)
    local_cols = jnp.arange(local.shape[1], dtype=jnp.int32)
    global_rows = (local_rows // width * row_devs + row_here) * width + local_rows % width
    global_cols = (local_cols // width * col_devs + col_here) * width + local_cols % width
    total = NPANEL * PW
    hi = lax.Precision.HIGH

    first_row = lax.all_gather(
        first_column[:width].astype(jnp.bfloat16), "fcol", axis=1, tiled=True
    )[:, :total]
    split = total // 2
    left = lax.all_gather(first_row[:, :split], "frow", axis=0, tiled=True)[:total]
    left, right_src, matrix = lax.optimization_barrier((left, first_row[:, split:], matrix))
    right = lax.all_gather(right_src, "frow", axis=0, tiled=True)[:total]
    right, own_column = lax.optimization_barrier((right, first_column))
    halves = [left.astype(jnp.float32), right.astype(jnp.float32)]
    row_panel = lax.all_gather(
        own_column.astype(jnp.bfloat16), "fcol", axis=1, tiled=True
    )[:, :total]
    half = row_devs // col_devs
    pairs = []
    for src_row in range(row_devs):
        for src_col in range(col_devs):
            dst_row = (src_row // col_devs) * col_devs + src_col
            dst_col = src_row % col_devs
            pairs.append((src_row * col_devs + src_col, dst_row * col_devs + dst_col))
    piece = lax.dynamic_slice_in_dim(row_panel, col_here * width, width, axis=0)
    piece = lax.ppermute(piece, ("frow", "fcol"), pairs)
    col_all = lax.all_gather(piece, "frow", axis=0, tiled=False)
    col_panel = (
        col_all.reshape(half, row_blocks, width, total)
        .transpose(1, 0, 2, 3)
        .reshape(local.shape[1], total)
    )
    rows_all = jnp.concatenate([row_panel, col_panel], axis=0).astype(jnp.float32)
    n_own = local.shape[0]
    full = lax.Precision.HIGHEST
    corner_blocks = total // width
    factor_full = jnp.zeros((total, total), jnp.float32)
    eye = jnp.eye(width, dtype=jnp.float32)
    inverses = []
    for h, cur in enumerate(halves):
        if h > 0:
            done_cols = factor_full[:, : h * split]
            cur = cur - jnp.dot(
                done_cols,
                done_cols[h * split : (h + 1) * split].T,
                precision=full,
                preferred_element_type=jnp.float32,
            )
        for b in range(split // width):
            start = h * split + b * width
            stop = start + width
            lb = b * width
            diag_block = cur[start:stop, lb : lb + width]
            symmetric = jnp.tril(diag_block) + jnp.tril(diag_block, -1).T
            factor = jnp.linalg.cholesky(symmetric)
            inverse = lax.linalg.triangular_solve(factor, eye, left_side=True, lower=True)
            inverses.append(inverse)
            factor_full = factor_full.at[start:stop, start:stop].set(factor)
            if stop < total:
                below = jnp.dot(
                    cur[stop:, lb : lb + width], inverse.T, precision=full, preferred_element_type=jnp.float32
                )
                factor_full = factor_full.at[stop:, start:stop].set(below)
                if lb + width < split:
                    cur = cur.at[stop:, lb + width :].add(
                        -jnp.dot(
                            below,
                            below[: split - lb - width].T,
                            precision=full,
                            preferred_element_type=jnp.float32,
                        )
                    )
    inv_blocks = jnp.stack(inverses)
    size = width
    while size < total:
        pairs_n = total // (2 * size)
        lower_left = jnp.stack(
            [
                factor_full[(2 * k + 1) * size : (2 * k + 2) * size, 2 * k * size : (2 * k + 1) * size]
                for k in range(pairs_n)
            ]
        )
        upper_inv = inv_blocks[0::2]
        lower_inv = inv_blocks[1::2]
        mixed = -jnp.einsum(
            "nab,nbc->nac",
            lower_inv,
            jnp.einsum("nab,nbc->nac", lower_left, upper_inv, precision=full),
            precision=full,
        )
        zeros = jnp.zeros_like(mixed)
        top = jnp.concatenate([upper_inv, zeros], axis=2)
        bottom = jnp.concatenate([mixed, lower_inv], axis=2)
        inv_blocks = jnp.concatenate([top, bottom], axis=1)
        size *= 2
    factor_inverse = inv_blocks[0]
    solved = jnp.dot(rows_all, factor_inverse.T, precision=hi, preferred_element_type=jnp.float32)
    row_factor = solved[:n_own]
    col_factor = solved[n_own:]
    matrix = subtract_product(matrix, row_factor, col_factor)
    corner_rows = lax.dynamic_slice_in_dim(
        factor_full, jnp.minimum(row_here, total // width - 1) * width, width, axis=0
    )
    head = jnp.where(row_here * width < total, corner_rows, row_factor[:width])
    panel_vals = jnp.concatenate([head, row_factor[width:]], axis=0)
    own_part = lax.dynamic_slice_in_dim(panel_vals, col_here * width, width, axis=1)
    matrix = matrix.at[:, :width].set(own_part)
    lower_part = global_rows[:, None] >= global_cols[None, :]
    result = jnp.where(lower_part, matrix, 0.0)
    return result[None, :, None, :]


def solution(mesh):
    return jax.shard_map(
        shards,
        mesh=mesh,
        in_specs=(
            P("frow", None, "fcol", None),
            P(("frow", "fcol"), None, None),
            P(("frow", "fcol"), None),
            P(("frow", "fcol"), None),
            P(("frow", "fcol"), None),
        ),
        out_specs=P("frow", None, "fcol", None),
        check_vma=False,
    )
```

```python
import jax
import jax.numpy as jnp
from jax import lax
from jax.sharding import PartitionSpec as P
from jax.experimental import pallas as pl

PW = 512
NPANEL = 2
CAP = 2


def as_sent(x):
    return jax.tree.map(lambda a: a.astype(jnp.bfloat16) if a.dtype == jnp.float32 else a, x)


def broadcast(block, axis, source):
    block = jnp.where(lax.axis_index(axis) == source, block, jnp.zeros_like(block))
    return lax.psum(block, axis)


def place_tiles(received):
    tile_block, perm_block, target_block = received
    width = tile_block.shape[-1]
    positions = jnp.arange(width, dtype=jnp.int32)
    row_onehot = (perm_block[:, :, 0, None, :] == positions[:, None]).astype(jnp.bfloat16)
    col_onehot = (perm_block[:, :, 1, None, :] == positions[:, None]).astype(jnp.bfloat16)
    moved = jnp.einsum(
        "abxi,abij->abxj", row_onehot, tile_block, preferred_element_type=jnp.float32
    ).astype(jnp.bfloat16)
    placed = jnp.einsum(
        "abxj,abyj->abxy", moved, col_onehot, preferred_element_type=jnp.float32
    ).astype(jnp.bfloat16)
    return (placed, target_block)


def subtract_product(matrix, row_factor, col_factor):
    product = jnp.dot(
        row_factor,
        col_factor.T,
        precision=lax.Precision.HIGH,
        preferred_element_type=jnp.float32,
    )
    return matrix - product


def _update_kernel(rows_ref, cols_ref, m_ref, r_ref, c_ref, o_ref):
    r = r_ref[...]
    c = c_ref[...]
    r_hi = r.astype(jnp.bfloat16)
    r_lo = (r - r_hi.astype(jnp.float32)).astype(jnp.bfloat16)
    c_hi = c.astype(jnp.bfloat16)
    c_lo = (c - c_hi.astype(jnp.float32)).astype(jnp.bfloat16)
    dims = (((1,), (1,)), ((), ()))
    acc = lax.dot_general(r_hi, c_hi, dims, preferred_element_type=jnp.float32)
    acc = acc + lax.dot_general(r_hi, c_lo, dims, preferred_element_type=jnp.float32)
    acc = acc + lax.dot_general(r_lo, c_hi, dims, preferred_element_type=jnp.float32)
    keep = rows_ref[...] >= cols_ref[...]
    o_ref[...] = jnp.where(keep, m_ref[...] - acc, 0.0)


def lower_update(matrix, row_factor, col_factor, global_rows, global_cols):
    n_rows, n_cols = matrix.shape
    depth = row_factor.shape[1]
    tm = 256
    tn = 512
    return pl.pallas_call(
        _update_kernel,
        grid=(n_rows // tm, n_cols // tn),
        in_specs=[
            pl.BlockSpec((tm, 1), lambda i, j: (i, 0)),
            pl.BlockSpec((1, tn), lambda i, j: (0, j)),
            pl.BlockSpec((tm, tn), lambda i, j: (i, j)),
            pl.BlockSpec((tm, depth), lambda i, j: (i, 0)),
            pl.BlockSpec((tn, depth), lambda i, j: (j, 0)),
        ],
        out_specs=pl.BlockSpec((tm, tn), lambda i, j: (i, j)),
        out_shape=jax.ShapeDtypeStruct(matrix.shape, jnp.float32),
    )(global_rows[:, None], global_cols[None, :], matrix, row_factor, col_factor)


def shards(front_orig, child_tiles, tile_target, tile_rows, tile_cols):
    row_devs = lax.axis_size("frow")
    col_devs = lax.axis_size("fcol")
    owners = row_devs * col_devs
    row_here = lax.axis_index("frow")
    col_here = lax.axis_index("fcol")
    width = child_tiles.shape[1]
    held = child_tiles.shape[0]
    slot_count = owners * CAP
    owner_of = tile_target[:, 0]
    block_of = tile_target[:, 1]
    tile_order = jnp.arange(held, dtype=jnp.int32)
    same_owner = owner_of[:, None] == owner_of[None, :]
    earlier = tile_order[None, :] < tile_order[:, None]
    rank_of = jnp.sum(jnp.where(same_owner & earlier, 1, 0), axis=1).astype(jnp.int32)
    slot_of = owner_of * CAP + rank_of
    slot_match = slot_of[None, :] == jnp.arange(slot_count, dtype=jnp.int32)[:, None]
    source_tile = jnp.sum(jnp.where(slot_match, tile_order[None, :], 0), axis=1)
    filled = jnp.any(slot_match, axis=1)
    own_perms = jnp.stack([tile_rows, tile_cols], axis=1)
    placed_here, _ = place_tiles((child_tiles[None], own_perms[None], block_of[None]))
    placed_here = placed_here[0]
    send_tiles = jnp.where(
        filled[:, None, None],
        jnp.take(placed_here, source_tile, axis=0),
        jnp.zeros((), jnp.bfloat16),
    )
    send_blocks = jnp.where(filled, jnp.take(block_of, source_tile, axis=0), -1)
    placed = lax.all_to_all(
        send_tiles.reshape(owners, CAP, width, width),
        ("frow", "fcol"),
        split_axis=0,
        concat_axis=0,
        tiled=True,
    )
    blocks_in = lax.all_to_all(
        send_blocks.reshape(owners, CAP),
        ("frow", "fcol"),
        split_axis=0,
        concat_axis=0,
        tiled=True,
    )
    local = front_orig[0, :, 0, :]
    row_blocks = local.shape[0] // width
    col_blocks = local.shape[1] // width
    block_ids = jnp.arange(row_blocks * col_blocks, dtype=jnp.int32)
    block_onehot = (blocks_in.reshape(1, slot_count) == block_ids[:, None]).astype(jnp.bfloat16)
    summed = jnp.dot(
        block_onehot, placed.reshape(slot_count, width * width), preferred_element_type=jnp.float32
    )
    added = (
        summed.reshape(row_blocks, col_blocks, width, width)
        .transpose(0, 2, 1, 3)
        .reshape(local.shape)
    )
    matrix = local + added
    first_ids = jnp.arange(row_blocks, dtype=jnp.int32) * col_blocks
    first_onehot = (blocks_in.reshape(1, slot_count) == first_ids[:, None]).astype(jnp.bfloat16)
    first_added = jnp.dot(
        first_onehot, placed.reshape(slot_count, width * width), preferred_element_type=jnp.float32
    ).reshape(local.shape[0], width)
    first_column = local[:, :width] + first_added
    local_rows = jnp.arange(local.shape[0], dtype=jnp.int32)
    local_cols = jnp.arange(local.shape[1], dtype=jnp.int32)
    global_rows = (local_rows // width * row_devs + row_here) * width + local_rows % width
    global_cols = (local_cols // width * col_devs + col_here) * width + local_cols % width
    total = NPANEL * PW
    hi = lax.Precision.HIGH

    first_row = lax.all_gather(
        first_column[:width].astype(jnp.bfloat16), "fcol", axis=1, tiled=True
    )[:, :total]
    split = total // 2
    left = lax.all_gather(first_row[:, :split], "frow", axis=0, tiled=True)[:total]
    left, right_src, matrix = lax.optimization_barrier((left, first_row[:, split:], matrix))
    right = lax.all_gather(right_src, "frow", axis=0, tiled=True)[:total]
    right, own_column = lax.optimization_barrier((right, first_column))
    halves = [left.astype(jnp.float32), right.astype(jnp.float32)]
    row_panel = lax.all_gather(
        own_column.astype(jnp.bfloat16), "fcol", axis=1, tiled=True
    )[:, :total]
    half = row_devs // col_devs
    pairs = []
    for src_row in range(row_devs):
        for src_col in range(col_devs):
            dst_row = (src_row // col_devs) * col_devs + src_col
            dst_col = src_row % col_devs
            pairs.append((src_row * col_devs + src_col, dst_row * col_devs + dst_col))
    piece = lax.dynamic_slice_in_dim(row_panel, col_here * width, width, axis=0)
    piece = lax.ppermute(piece, ("frow", "fcol"), pairs)
    col_all = lax.all_gather(piece, "frow", axis=0, tiled=False)
    col_panel = (
        col_all.reshape(half, row_blocks, width, total)
        .transpose(1, 0, 2, 3)
        .reshape(local.shape[1], total)
    )
    rows_all = jnp.concatenate([row_panel, col_panel], axis=0).astype(jnp.float32)
    n_own = local.shape[0]
    full = lax.Precision.HIGHEST
    corner_blocks = total // width
    factor_full = jnp.zeros((total, total), jnp.float32)
    eye = jnp.eye(width, dtype=jnp.float32)
    inverses = []
    for h, cur in enumerate(halves):
        if h > 0:
            done_cols = factor_full[:, : h * split]
            cur = cur - jnp.dot(
                done_cols,
                done_cols[h * split : (h + 1) * split].T,
                precision=full,
                preferred_element_type=jnp.float32,
            )
        for b in range(split // width):
            start = h * split + b * width
            stop = start + width
            lb = b * width
            diag_block = cur[start:stop, lb : lb + width]
            symmetric = jnp.tril(diag_block) + jnp.tril(diag_block, -1).T
            factor = jnp.linalg.cholesky(symmetric)
            inverse = lax.linalg.triangular_solve(factor, eye, left_side=True, lower=True)
            inverses.append(inverse)
            factor_full = factor_full.at[start:stop, start:stop].set(factor)
            if stop < total:
                below = jnp.dot(
                    cur[stop:, lb : lb + width], inverse.T, precision=full, preferred_element_type=jnp.float32
                )
                factor_full = factor_full.at[stop:, start:stop].set(below)
                if lb + width < split:
                    cur = cur.at[stop:, lb + width :].add(
                        -jnp.dot(
                            below,
                            below[: split - lb - width].T,
                            precision=full,
                            preferred_element_type=jnp.float32,
                        )
                    )
    inv_blocks = jnp.stack(inverses)
    size = width
    while size < total:
        pairs_n = total // (2 * size)
        lower_left = jnp.stack(
            [
                factor_full[(2 * k + 1) * size : (2 * k + 2) * size, 2 * k * size : (2 * k + 1) * size]
                for k in range(pairs_n)
            ]
        )
        upper_inv = inv_blocks[0::2]
        lower_inv = inv_blocks[1::2]
        mixed = -jnp.einsum(
            "nab,nbc->nac",
            lower_inv,
            jnp.einsum("nab,nbc->nac", lower_left, upper_inv, precision=full),
            precision=full,
        )
        zeros = jnp.zeros_like(mixed)
        top = jnp.concatenate([upper_inv, zeros], axis=2)
        bottom = jnp.concatenate([mixed, lower_inv], axis=2)
        inv_blocks = jnp.concatenate([top, bottom], axis=1)
        size *= 2
    factor_inverse = inv_blocks[0]
    solved = jnp.dot(rows_all, factor_inverse.T, precision=hi, preferred_element_type=jnp.float32)
    row_factor = solved[:n_own]
    col_factor = solved[n_own:]
    matrix = lower_update(matrix, row_factor, col_factor, global_rows, global_cols)
    corner_rows = lax.dynamic_slice_in_dim(
        factor_full, jnp.minimum(row_here, total // width - 1) * width, width, axis=0
    )
    head = jnp.where(row_here * width < total, corner_rows, row_factor[:width])
    panel_vals = jnp.concatenate([head, row_factor[width:]], axis=0)
    own_part = lax.dynamic_slice_in_dim(panel_vals, col_here * width, width, axis=1)
    result = matrix.at[:, :width].set(own_part)
    return result[None, :, None, :]


def solution(mesh):
    return jax.shard_map(
        shards,
        mesh=mesh,
        in_specs=(
            P("frow", None, "fcol", None),
            P(("frow", "fcol"), None, None),
            P(("frow", "fcol"), None),
            P(("frow", "fcol"), None),
            P(("frow", "fcol"), None),
        ),
        out_specs=P("frow", None, "fcol", None),
        check_vma=False,
    )
```

```python
import jax
import jax.numpy as jnp
from jax import lax
from jax.sharding import PartitionSpec as P
from jax.experimental import pallas as pl

PW = 512
NPANEL = 2
CAP = 2


def as_sent(x):
    return jax.tree.map(lambda a: a.astype(jnp.bfloat16) if a.dtype == jnp.float32 else a, x)


def broadcast(block, axis, source):
    block = jnp.where(lax.axis_index(axis) == source, block, jnp.zeros_like(block))
    return lax.psum(block, axis)


def place_tiles(received):
    tile_block, perm_block, target_block = received
    width = tile_block.shape[-1]
    positions = jnp.arange(width, dtype=jnp.int32)
    row_onehot = (perm_block[:, :, 0, None, :] == positions[:, None]).astype(jnp.bfloat16)
    col_onehot = (perm_block[:, :, 1, None, :] == positions[:, None]).astype(jnp.bfloat16)
    moved = jnp.einsum(
        "abxi,abij->abxj", row_onehot, tile_block, preferred_element_type=jnp.float32
    ).astype(jnp.bfloat16)
    placed = jnp.einsum(
        "abxj,abyj->abxy", moved, col_onehot, preferred_element_type=jnp.float32
    ).astype(jnp.bfloat16)
    return (placed, target_block)


def subtract_product(matrix, row_factor, col_factor):
    product = jnp.dot(
        row_factor,
        col_factor.T,
        precision=lax.Precision.HIGH,
        preferred_element_type=jnp.float32,
    )
    return matrix - product


def _update_kernel(rows_ref, cols_ref, m_ref, rh_ref, rl_ref, ch_ref, cl_ref, o_ref):
    dims = (((1,), (1,)), ((), ()))
    r_hi = rh_ref[...]
    c_hi = ch_ref[...]
    acc = lax.dot_general(r_hi, c_hi, dims, preferred_element_type=jnp.float32)
    acc = acc + lax.dot_general(r_hi, cl_ref[...], dims, preferred_element_type=jnp.float32)
    acc = acc + lax.dot_general(rl_ref[...], c_hi, dims, preferred_element_type=jnp.float32)
    keep = rows_ref[...] >= cols_ref[...]
    o_ref[...] = jnp.where(keep, m_ref[...] - acc, 0.0)


def split_bf16(x):
    hi = x.astype(jnp.bfloat16)
    return hi, (x - hi.astype(jnp.float32)).astype(jnp.bfloat16)


def lower_update(matrix, row_factor, col_factor, global_rows, global_cols):
    n_rows, n_cols = matrix.shape
    depth = row_factor.shape[1]
    tm = 512
    tn = 512
    r_hi, r_lo = split_bf16(row_factor)
    c_hi, c_lo = split_bf16(col_factor)
    row_spec = pl.BlockSpec((tm, depth), lambda i, j: (i, 0))
    col_spec = pl.BlockSpec((tn, depth), lambda i, j: (j, 0))
    return pl.pallas_call(
        _update_kernel,
        grid=(n_rows // tm, n_cols // tn),
        in_specs=[
            pl.BlockSpec((tm, 1), lambda i, j: (i, 0)),
            pl.BlockSpec((1, tn), lambda i, j: (0, j)),
            pl.BlockSpec((tm, tn), lambda i, j: (i, j)),
            row_spec,
            row_spec,
            col_spec,
            col_spec,
        ],
        out_specs=pl.BlockSpec((tm, tn), lambda i, j: (i, j)),
        out_shape=jax.ShapeDtypeStruct(matrix.shape, jnp.float32),
    )(global_rows[:, None], global_cols[None, :], matrix, r_hi, r_lo, c_hi, c_lo)


def shards(front_orig, child_tiles, tile_target, tile_rows, tile_cols):
    row_devs = lax.axis_size("frow")
    col_devs = lax.axis_size("fcol")
    owners = row_devs * col_devs
    row_here = lax.axis_index("frow")
    col_here = lax.axis_index("fcol")
    width = child_tiles.shape[1]
    held = child_tiles.shape[0]
    slot_count = owners * CAP
    owner_of = tile_target[:, 0]
    block_of = tile_target[:, 1]
    tile_order = jnp.arange(held, dtype=jnp.int32)
    same_owner = owner_of[:, None] == owner_of[None, :]
    earlier = tile_order[None, :] < tile_order[:, None]
    rank_of = jnp.sum(jnp.where(same_owner & earlier, 1, 0), axis=1).astype(jnp.int32)
    slot_of = owner_of * CAP + rank_of
    slot_match = slot_of[None, :] == jnp.arange(slot_count, dtype=jnp.int32)[:, None]
    source_tile = jnp.sum(jnp.where(slot_match, tile_order[None, :], 0), axis=1)
    filled = jnp.any(slot_match, axis=1)
    own_perms = jnp.stack([tile_rows, tile_cols], axis=1)
    placed_here, _ = place_tiles((child_tiles[None], own_perms[None], block_of[None]))
    placed_here = placed_here[0]
    send_tiles = jnp.where(
        filled[:, None, None],
        jnp.take(placed_here, source_tile, axis=0),
        jnp.zeros((), jnp.bfloat16),
    )
    send_blocks = jnp.where(filled, jnp.take(block_of, source_tile, axis=0), -1)
    placed = lax.all_to_all(
        send_tiles.reshape(owners, CAP, width, width),
        ("frow", "fcol"),
        split_axis=0,
        concat_axis=0,
        tiled=True,
    )
    blocks_in = lax.all_to_all(
        send_blocks.reshape(owners, CAP),
        ("frow", "fcol"),
        split_axis=0,
        concat_axis=0,
        tiled=True,
    )
    local = front_orig[0, :, 0, :]
    row_blocks = local.shape[0] // width
    col_blocks = local.shape[1] // width
    block_ids = jnp.arange(row_blocks * col_blocks, dtype=jnp.int32)
    block_onehot = (blocks_in.reshape(1, slot_count) == block_ids[:, None]).astype(jnp.bfloat16)
    summed = jnp.dot(
        block_onehot, placed.reshape(slot_count, width * width), preferred_element_type=jnp.float32
    )
    added = (
        summed.reshape(row_blocks, col_blocks, width, width)
        .transpose(0, 2, 1, 3)
        .reshape(local.shape)
    )
    matrix = local + added
    first_ids = jnp.arange(row_blocks, dtype=jnp.int32) * col_blocks
    first_onehot = (blocks_in.reshape(1, slot_count) == first_ids[:, None]).astype(jnp.bfloat16)
    first_added = jnp.dot(
        first_onehot, placed.reshape(slot_count, width * width), preferred_element_type=jnp.float32
    ).reshape(local.shape[0], width)
    first_column = local[:, :width] + first_added
    local_rows = jnp.arange(local.shape[0], dtype=jnp.int32)
    local_cols = jnp.arange(local.shape[1], dtype=jnp.int32)
    global_rows = (local_rows // width * row_devs + row_here) * width + local_rows % width
    global_cols = (local_cols // width * col_devs + col_here) * width + local_cols % width
    total = NPANEL * PW
    hi = lax.Precision.HIGH

    first_row = lax.all_gather(
        first_column[:width].astype(jnp.bfloat16), "fcol", axis=1, tiled=True
    )[:, :total]
    split = total // 2
    left = lax.all_gather(first_row[:, :split], "frow", axis=0, tiled=True)[:total]
    left, right_src, matrix = lax.optimization_barrier((left, first_row[:, split:], matrix))
    right = lax.all_gather(right_src, "frow", axis=0, tiled=True)[:total]
    right, own_column = lax.optimization_barrier((right, first_column))
    halves = [left.astype(jnp.float32), right.astype(jnp.float32)]
    row_panel = lax.all_gather(
        own_column.astype(jnp.bfloat16), "fcol", axis=1, tiled=True
    )[:, :total]
    half = row_devs // col_devs
    pairs = []
    for src_row in range(row_devs):
        for src_col in range(col_devs):
            dst_row = (src_row // col_devs) * col_devs + src_col
            dst_col = src_row % col_devs
            pairs.append((src_row * col_devs + src_col, dst_row * col_devs + dst_col))
    piece = lax.dynamic_slice_in_dim(row_panel, col_here * width, width, axis=0)
    piece = lax.ppermute(piece, ("frow", "fcol"), pairs)
    col_all = lax.all_gather(piece, "frow", axis=0, tiled=False)
    col_panel = (
        col_all.reshape(half, row_blocks, width, total)
        .transpose(1, 0, 2, 3)
        .reshape(local.shape[1], total)
    )
    rows_all = jnp.concatenate([row_panel, col_panel], axis=0).astype(jnp.float32)
    n_own = local.shape[0]
    full = lax.Precision.HIGHEST
    corner_blocks = total // width
    factor_full = jnp.zeros((total, total), jnp.float32)
    eye = jnp.eye(width, dtype=jnp.float32)
    inverses = []
    for h, cur in enumerate(halves):
        if h > 0:
            done_cols = factor_full[:, : h * split]
            cur = cur - jnp.dot(
                done_cols,
                done_cols[h * split : (h + 1) * split].T,
                precision=full,
                preferred_element_type=jnp.float32,
            )
        for b in range(split // width):
            start = h * split + b * width
            stop = start + width
            lb = b * width
            diag_block = cur[start:stop, lb : lb + width]
            symmetric = jnp.tril(diag_block) + jnp.tril(diag_block, -1).T
            factor = jnp.linalg.cholesky(symmetric)
            inverse = lax.linalg.triangular_solve(factor, eye, left_side=True, lower=True)
            inverses.append(inverse)
            factor_full = factor_full.at[start:stop, start:stop].set(factor)
            if stop < total:
                below = jnp.dot(
                    cur[stop:, lb : lb + width], inverse.T, precision=full, preferred_element_type=jnp.float32
                )
                factor_full = factor_full.at[stop:, start:stop].set(below)
                if lb + width < split:
                    cur = cur.at[stop:, lb + width :].add(
                        -jnp.dot(
                            below,
                            below[: split - lb - width].T,
                            precision=full,
                            preferred_element_type=jnp.float32,
                        )
                    )
    inv_blocks = jnp.stack(inverses)
    size = width
    while size < total:
        pairs_n = total // (2 * size)
        lower_left = jnp.stack(
            [
                factor_full[(2 * k + 1) * size : (2 * k + 2) * size, 2 * k * size : (2 * k + 1) * size]
                for k in range(pairs_n)
            ]
        )
        upper_inv = inv_blocks[0::2]
        lower_inv = inv_blocks[1::2]
        mixed = -jnp.einsum(
            "nab,nbc->nac",
            lower_inv,
            jnp.einsum("nab,nbc->nac", lower_left, upper_inv, precision=full),
            precision=full,
        )
        zeros = jnp.zeros_like(mixed)
        top = jnp.concatenate([upper_inv, zeros], axis=2)
        bottom = jnp.concatenate([mixed, lower_inv], axis=2)
        inv_blocks = jnp.concatenate([top, bottom], axis=1)
        size *= 2
    factor_inverse = inv_blocks[0]
    solved = jnp.dot(rows_all, factor_inverse.T, precision=hi, preferred_element_type=jnp.float32)
    row_factor = solved[:n_own]
    col_factor = solved[n_own:]
    matrix = lower_update(matrix, row_factor, col_factor, global_rows, global_cols)
    corner_rows = lax.dynamic_slice_in_dim(
        factor_full, jnp.minimum(row_here, total // width - 1) * width, width, axis=0
    )
    head = jnp.where(row_here * width < total, corner_rows, row_factor[:width])
    panel_vals = jnp.concatenate([head, row_factor[width:]], axis=0)
    own_part = lax.dynamic_slice_in_dim(panel_vals, col_here * width, width, axis=1)
    result = matrix.at[:, :width].set(own_part)
    return result[None, :, None, :]


def solution(mesh):
    return jax.shard_map(
        shards,
        mesh=mesh,
        in_specs=(
            P("frow", None, "fcol", None),
            P(("frow", "fcol"), None, None),
            P(("frow", "fcol"), None),
            P(("frow", "fcol"), None),
            P(("frow", "fcol"), None),
        ),
        out_specs=P("frow", None, "fcol", None),
        check_vma=False,
    )
```

```python
import jax
import jax.numpy as jnp
from jax import lax
from jax.sharding import PartitionSpec as P
from jax.experimental import pallas as pl

PW = 512
NPANEL = 2
CAP = 2


def as_sent(x):
    return jax.tree.map(lambda a: a.astype(jnp.bfloat16) if a.dtype == jnp.float32 else a, x)


def broadcast(block, axis, source):
    block = jnp.where(lax.axis_index(axis) == source, block, jnp.zeros_like(block))
    return lax.psum(block, axis)


def place_tiles(received):
    tile_block, perm_block, target_block = received
    width = tile_block.shape[-1]
    positions = jnp.arange(width, dtype=jnp.int32)
    row_onehot = (perm_block[:, :, 0, None, :] == positions[:, None]).astype(jnp.bfloat16)
    col_onehot = (perm_block[:, :, 1, None, :] == positions[:, None]).astype(jnp.bfloat16)
    moved = jnp.einsum(
        "abxi,abij->abxj", row_onehot, tile_block, preferred_element_type=jnp.float32
    ).astype(jnp.bfloat16)
    placed = jnp.einsum(
        "abxj,abyj->abxy", moved, col_onehot, preferred_element_type=jnp.float32
    ).astype(jnp.bfloat16)
    return (placed, target_block)


def subtract_product(matrix, row_factor, col_factor):
    product = jnp.dot(
        row_factor,
        col_factor.T,
        precision=lax.Precision.HIGH,
        preferred_element_type=jnp.float32,
    )
    return matrix - product


def _update_kernel(rows_ref, cols_ref, m_ref, rh_ref, rl_ref, ch_ref, cl_ref, panel_ref, o_ref):
    dims = (((1,), (1,)), ((), ()))
    r_hi = rh_ref[...]
    c_hi = ch_ref[...]
    acc = lax.dot_general(r_hi, c_hi, dims, preferred_element_type=jnp.float32)
    acc = acc + lax.dot_general(r_hi, cl_ref[...], dims, preferred_element_type=jnp.float32)
    acc = acc + lax.dot_general(rl_ref[...], c_hi, dims, preferred_element_type=jnp.float32)
    keep = rows_ref[...] >= cols_ref[...]
    o_ref[...] = jnp.where(keep, m_ref[...] - acc, 0.0)

    @pl.when(pl.program_id(1) == 0)
    def _():
        o_ref[:, : panel_ref.shape[1]] = panel_ref[...]


def split_bf16(x):
    hi = x.astype(jnp.bfloat16)
    return hi, (x - hi.astype(jnp.float32)).astype(jnp.bfloat16)


def lower_update(matrix, row_factor, col_factor, global_rows, global_cols, panel):
    n_rows, n_cols = matrix.shape
    depth = row_factor.shape[1]
    tm = 512
    tn = 512
    r_hi, r_lo = split_bf16(row_factor)
    c_hi, c_lo = split_bf16(col_factor)
    row_spec = pl.BlockSpec((tm, depth), lambda i, j: (i, 0))
    col_spec = pl.BlockSpec((tn, depth), lambda i, j: (j, 0))
    return pl.pallas_call(
        _update_kernel,
        grid=(n_rows // tm, n_cols // tn),
        in_specs=[
            pl.BlockSpec((tm, 1), lambda i, j: (i, 0)),
            pl.BlockSpec((1, tn), lambda i, j: (0, j)),
            pl.BlockSpec((tm, tn), lambda i, j: (i, j)),
            row_spec,
            row_spec,
            col_spec,
            col_spec,
            pl.BlockSpec((tm, panel.shape[1]), lambda i, j: (i, 0)),
        ],
        out_specs=pl.BlockSpec((tm, tn), lambda i, j: (i, j)),
        out_shape=jax.ShapeDtypeStruct(matrix.shape, jnp.float32),
    )(global_rows[:, None], global_cols[None, :], matrix, r_hi, r_lo, c_hi, c_lo, panel)


def shards(front_orig, child_tiles, tile_target, tile_rows, tile_cols):
    row_devs = lax.axis_size("frow")
    col_devs = lax.axis_size("fcol")
    owners = row_devs * col_devs
    row_here = lax.axis_index("frow")
    col_here = lax.axis_index("fcol")
    width = child_tiles.shape[1]
    held = child_tiles.shape[0]
    slot_count = owners * CAP
    owner_of = tile_target[:, 0]
    block_of = tile_target[:, 1]
    tile_order = jnp.arange(held, dtype=jnp.int32)
    same_owner = owner_of[:, None] == owner_of[None, :]
    earlier = tile_order[None, :] < tile_order[:, None]
    rank_of = jnp.sum(jnp.where(same_owner & earlier, 1, 0), axis=1).astype(jnp.int32)
    slot_of = owner_of * CAP + rank_of
    slot_match = slot_of[None, :] == jnp.arange(slot_count, dtype=jnp.int32)[:, None]
    source_tile = jnp.sum(jnp.where(slot_match, tile_order[None, :], 0), axis=1)
    filled = jnp.any(slot_match, axis=1)
    own_perms = jnp.stack([tile_rows, tile_cols], axis=1)
    placed_here, _ = place_tiles((child_tiles[None], own_perms[None], block_of[None]))
    placed_here = placed_here[0]
    send_tiles = jnp.where(
        filled[:, None, None],
        jnp.take(placed_here, source_tile, axis=0),
        jnp.zeros((), jnp.bfloat16),
    )
    send_blocks = jnp.where(filled, jnp.take(block_of, source_tile, axis=0), -1)
    placed = lax.all_to_all(
        send_tiles.reshape(owners, CAP, width, width),
        ("frow", "fcol"),
        split_axis=0,
        concat_axis=0,
        tiled=True,
    )
    blocks_in = lax.all_to_all(
        send_blocks.reshape(owners, CAP),
        ("frow", "fcol"),
        split_axis=0,
        concat_axis=0,
        tiled=True,
    )
    local = front_orig[0, :, 0, :]
    row_blocks = local.shape[0] // width
    col_blocks = local.shape[1] // width
    block_ids = jnp.arange(row_blocks * col_blocks, dtype=jnp.int32)
    block_onehot = (blocks_in.reshape(1, slot_count) == block_ids[:, None]).astype(jnp.bfloat16)
    summed = jnp.dot(
        block_onehot, placed.reshape(slot_count, width * width), preferred_element_type=jnp.float32
    )
    added = (
        summed.reshape(row_blocks, col_blocks, width, width)
        .transpose(0, 2, 1, 3)
        .reshape(local.shape)
    )
    matrix = local + added
    first_ids = jnp.arange(row_blocks, dtype=jnp.int32) * col_blocks
    first_onehot = (blocks_in.reshape(1, slot_count) == first_ids[:, None]).astype(jnp.bfloat16)
    first_added = jnp.dot(
        first_onehot, placed.reshape(slot_count, width * width), preferred_element_type=jnp.float32
    ).reshape(local.shape[0], width)
    first_column = local[:, :width] + first_added
    local_rows = jnp.arange(local.shape[0], dtype=jnp.int32)
    local_cols = jnp.arange(local.shape[1], dtype=jnp.int32)
    global_rows = (local_rows // width * row_devs + row_here) * width + local_rows % width
    global_cols = (local_cols // width * col_devs + col_here) * width + local_cols % width
    total = NPANEL * PW
    hi = lax.Precision.HIGH

    first_row = lax.all_gather(
        first_column[:width].astype(jnp.bfloat16), "fcol", axis=1, tiled=True
    )[:, :total]
    split = total // 2
    left = lax.all_gather(first_row[:, :split], "frow", axis=0, tiled=True)[:total]
    left, right_src, matrix = lax.optimization_barrier((left, first_row[:, split:], matrix))
    right = lax.all_gather(right_src, "frow", axis=0, tiled=True)[:total]
    right, own_column = lax.optimization_barrier((right, first_column))
    halves = [left.astype(jnp.float32), right.astype(jnp.float32)]
    row_panel = lax.all_gather(
        own_column.astype(jnp.bfloat16), "fcol", axis=1, tiled=True
    )[:, :total]
    half = row_devs // col_devs
    pairs = []
    for src_row in range(row_devs):
        for src_col in range(col_devs):
            dst_row = (src_row // col_devs) * col_devs + src_col
            dst_col = src_row % col_devs
            pairs.append((src_row * col_devs + src_col, dst_row * col_devs + dst_col))
    piece = lax.dynamic_slice_in_dim(row_panel, col_here * width, width, axis=0)
    piece = lax.ppermute(piece, ("frow", "fcol"), pairs)
    col_all = lax.all_gather(piece, "frow", axis=0, tiled=False)
    col_panel = (
        col_all.reshape(half, row_blocks, width, total)
        .transpose(1, 0, 2, 3)
        .reshape(local.shape[1], total)
    )
    rows_all = jnp.concatenate([row_panel, col_panel], axis=0).astype(jnp.float32)
    n_own = local.shape[0]
    full = lax.Precision.HIGHEST
    corner_blocks = total // width
    factor_full = jnp.zeros((total, total), jnp.float32)
    eye = jnp.eye(width, dtype=jnp.float32)
    inverses = []
    for h, cur in enumerate(halves):
        if h > 0:
            done_cols = factor_full[:, : h * split]
            cur = cur - jnp.dot(
                done_cols,
                done_cols[h * split : (h + 1) * split].T,
                precision=full,
                preferred_element_type=jnp.float32,
            )
        for b in range(split // width):
            start = h * split + b * width
            stop = start + width
            lb = b * width
            diag_block = cur[start:stop, lb : lb + width]
            symmetric = jnp.tril(diag_block) + jnp.tril(diag_block, -1).T
            factor = jnp.linalg.cholesky(symmetric)
            inverse = lax.linalg.triangular_solve(factor, eye, left_side=True, lower=True)
            inverses.append(inverse)
            factor_full = factor_full.at[start:stop, start:stop].set(factor)
            if stop < total:
                below = jnp.dot(
                    cur[stop:, lb : lb + width], inverse.T, precision=full, preferred_element_type=jnp.float32
                )
                factor_full = factor_full.at[stop:, start:stop].set(below)
                if lb + width < split:
                    cur = cur.at[stop:, lb + width :].add(
                        -jnp.dot(
                            below,
                            below[: split - lb - width].T,
                            precision=full,
                            preferred_element_type=jnp.float32,
                        )
                    )
    inv_blocks = jnp.stack(inverses)
    size = width
    while size < total:
        pairs_n = total // (2 * size)
        lower_left = jnp.stack(
            [
                factor_full[(2 * k + 1) * size : (2 * k + 2) * size, 2 * k * size : (2 * k + 1) * size]
                for k in range(pairs_n)
            ]
        )
        upper_inv = inv_blocks[0::2]
        lower_inv = inv_blocks[1::2]
        mixed = -jnp.einsum(
            "nab,nbc->nac",
            lower_inv,
            jnp.einsum("nab,nbc->nac", lower_left, upper_inv, precision=full),
            precision=full,
        )
        zeros = jnp.zeros_like(mixed)
        top = jnp.concatenate([upper_inv, zeros], axis=2)
        bottom = jnp.concatenate([mixed, lower_inv], axis=2)
        inv_blocks = jnp.concatenate([top, bottom], axis=1)
        size *= 2
    factor_inverse = inv_blocks[0]
    solved = jnp.dot(rows_all, factor_inverse.T, precision=hi, preferred_element_type=jnp.float32)
    row_factor = solved[:n_own]
    col_factor = solved[n_own:]
    corner_rows = lax.dynamic_slice_in_dim(
        factor_full, jnp.minimum(row_here, total // width - 1) * width, width, axis=0
    )
    head = jnp.where(row_here * width < total, corner_rows, row_factor[:width])
    panel_vals = jnp.concatenate([head, row_factor[width:]], axis=0)
    own_part = lax.dynamic_slice_in_dim(panel_vals, col_here * width, width, axis=1)
    result = lower_update(matrix, row_factor, col_factor, global_rows, global_cols, own_part)
    return result[None, :, None, :]


def solution(mesh):
    return jax.shard_map(
        shards,
        mesh=mesh,
        in_specs=(
            P("frow", None, "fcol", None),
            P(("frow", "fcol"), None, None),
            P(("frow", "fcol"), None),
            P(("frow", "fcol"), None),
            P(("frow", "fcol"), None),
        ),
        out_specs=P("frow", None, "fcol", None),
        check_vma=False,
    )
```

```python
import jax
import jax.numpy as jnp
from jax import lax
from jax.sharding import PartitionSpec as P
from jax.experimental import pallas as pl

PW = 512
NPANEL = 2
CAP = 2


def as_sent(x):
    return jax.tree.map(lambda a: a.astype(jnp.bfloat16) if a.dtype == jnp.float32 else a, x)


def broadcast(block, axis, source):
    block = jnp.where(lax.axis_index(axis) == source, block, jnp.zeros_like(block))
    return lax.psum(block, axis)


def place_tiles(received):
    tile_block, perm_block, target_block = received
    width = tile_block.shape[-1]
    positions = jnp.arange(width, dtype=jnp.int32)
    row_onehot = (perm_block[:, :, 0, None, :] == positions[:, None]).astype(jnp.bfloat16)
    col_onehot = (perm_block[:, :, 1, None, :] == positions[:, None]).astype(jnp.bfloat16)
    moved = jnp.einsum(
        "abxi,abij->abxj", row_onehot, tile_block, preferred_element_type=jnp.float32
    ).astype(jnp.bfloat16)
    placed = jnp.einsum(
        "abxj,abyj->abxy", moved, col_onehot, preferred_element_type=jnp.float32
    ).astype(jnp.bfloat16)
    return (placed, target_block)


def subtract_product(matrix, row_factor, col_factor):
    product = jnp.dot(
        row_factor,
        col_factor.T,
        precision=lax.Precision.HIGH,
        preferred_element_type=jnp.float32,
    )
    return matrix - product


def _update_kernel(rows_ref, cols_ref, m_ref, rh_ref, rl_ref, ch_ref, cl_ref, panel_ref, o_ref):
    dims = (((1,), (1,)), ((), ()))
    r_hi = rh_ref[...]
    c_hi = ch_ref[...]
    acc = lax.dot_general(r_hi, c_hi, dims, preferred_element_type=jnp.float32)
    acc = acc + lax.dot_general(r_hi, cl_ref[...], dims, preferred_element_type=jnp.float32)
    acc = acc + lax.dot_general(rl_ref[...], c_hi, dims, preferred_element_type=jnp.float32)
    keep = rows_ref[...] >= cols_ref[...]
    o_ref[...] = jnp.where(keep, m_ref[...] - acc, 0.0)

    @pl.when(pl.program_id(1) == 0)
    def _():
        o_ref[:, : panel_ref.shape[1]] = panel_ref[...]


def split_bf16(x):
    hi = x.astype(jnp.bfloat16)
    return hi, (x - hi.astype(jnp.float32)).astype(jnp.bfloat16)


def lower_update(matrix, row_factor, col_factor, global_rows, global_cols, panel):
    n_rows, n_cols = matrix.shape
    depth = row_factor.shape[1]
    tm = 512
    tn = 1024
    r_hi, r_lo = split_bf16(row_factor)
    c_hi, c_lo = split_bf16(col_factor)
    row_spec = pl.BlockSpec((tm, depth), lambda i, j: (i, 0))
    col_spec = pl.BlockSpec((tn, depth), lambda i, j: (j, 0))
    return pl.pallas_call(
        _update_kernel,
        grid=(n_rows // tm, n_cols // tn),
        in_specs=[
            pl.BlockSpec((tm, 1), lambda i, j: (i, 0)),
            pl.BlockSpec((1, tn), lambda i, j: (0, j)),
            pl.BlockSpec((tm, tn), lambda i, j: (i, j)),
            row_spec,
            row_spec,
            col_spec,
            col_spec,
            pl.BlockSpec((tm, panel.shape[1]), lambda i, j: (i, 0)),
        ],
        out_specs=pl.BlockSpec((tm, tn), lambda i, j: (i, j)),
        out_shape=jax.ShapeDtypeStruct(matrix.shape, jnp.float32),
    )(global_rows[:, None], global_cols[None, :], matrix, r_hi, r_lo, c_hi, c_lo, panel)


def shards(front_orig, child_tiles, tile_target, tile_rows, tile_cols):
    row_devs = lax.axis_size("frow")
    col_devs = lax.axis_size("fcol")
    owners = row_devs * col_devs
    row_here = lax.axis_index("frow")
    col_here = lax.axis_index("fcol")
    width = child_tiles.shape[1]
    held = child_tiles.shape[0]
    slot_count = owners * CAP
    owner_of = tile_target[:, 0]
    block_of = tile_target[:, 1]
    tile_order = jnp.arange(held, dtype=jnp.int32)
    same_owner = owner_of[:, None] == owner_of[None, :]
    earlier = tile_order[None, :] < tile_order[:, None]
    rank_of = jnp.sum(jnp.where(same_owner & earlier, 1, 0), axis=1).astype(jnp.int32)
    slot_of = owner_of * CAP + rank_of
    slot_match = slot_of[None, :] == jnp.arange(slot_count, dtype=jnp.int32)[:, None]
    source_tile = jnp.sum(jnp.where(slot_match, tile_order[None, :], 0), axis=1)
    filled = jnp.any(slot_match, axis=1)
    own_perms = jnp.stack([tile_rows, tile_cols], axis=1)
    placed_here, _ = place_tiles((child_tiles[None], own_perms[None], block_of[None]))
    placed_here = placed_here[0]
    send_tiles = jnp.where(
        filled[:, None, None],
        jnp.take(placed_here, source_tile, axis=0),
        jnp.zeros((), jnp.bfloat16),
    )
    send_blocks = jnp.where(filled, jnp.take(block_of, source_tile, axis=0), -1)
    placed = lax.all_to_all(
        send_tiles.reshape(owners, CAP, width, width),
        ("frow", "fcol"),
        split_axis=0,
        concat_axis=0,
        tiled=True,
    )
    blocks_in = lax.all_to_all(
        send_blocks.reshape(owners, CAP),
        ("frow", "fcol"),
        split_axis=0,
        concat_axis=0,
        tiled=True,
    )
    local = front_orig[0, :, 0, :]
    row_blocks = local.shape[0] // width
    col_blocks = local.shape[1] // width
    block_ids = jnp.arange(row_blocks * col_blocks, dtype=jnp.int32)
    block_onehot = (blocks_in.reshape(1, slot_count) == block_ids[:, None]).astype(jnp.bfloat16)
    summed = jnp.dot(
        block_onehot, placed.reshape(slot_count, width * width), preferred_element_type=jnp.float32
    )
    added = (
        summed.reshape(row_blocks, col_blocks, width, width)
        .transpose(0, 2, 1, 3)
        .reshape(local.shape)
    )
    matrix = local + added
    first_ids = jnp.arange(row_blocks, dtype=jnp.int32) * col_blocks
    first_onehot = (blocks_in.reshape(1, slot_count) == first_ids[:, None]).astype(jnp.bfloat16)
    first_added = jnp.dot(
        first_onehot, placed.reshape(slot_count, width * width), preferred_element_type=jnp.float32
    ).reshape(local.shape[0], width)
    first_column = local[:, :width] + first_added
    local_rows = jnp.arange(local.shape[0], dtype=jnp.int32)
    local_cols = jnp.arange(local.shape[1], dtype=jnp.int32)
    global_rows = (local_rows // width * row_devs + row_here) * width + local_rows % width
    global_cols = (local_cols // width * col_devs + col_here) * width + local_cols % width
    total = NPANEL * PW
    hi = lax.Precision.HIGH

    first_row = lax.all_gather(
        first_column[:width].astype(jnp.bfloat16), "fcol", axis=1, tiled=True
    )[:, :total]
    split = total // 2
    left = lax.all_gather(first_row[:, :split], "frow", axis=0, tiled=True)[:total]
    left, right_src, matrix = lax.optimization_barrier((left, first_row[:, split:], matrix))
    right = lax.all_gather(right_src, "frow", axis=0, tiled=True)[:total]
    right, own_column = lax.optimization_barrier((right, first_column))
    halves = [left.astype(jnp.float32), right.astype(jnp.float32)]
    row_panel = lax.all_gather(
        own_column.astype(jnp.bfloat16), "fcol", axis=1, tiled=True
    )[:, :total]
    half = row_devs // col_devs
    pairs = []
    for src_row in range(row_devs):
        for src_col in range(col_devs):
            dst_row = (src_row // col_devs) * col_devs + src_col
            dst_col = src_row % col_devs
            pairs.append((src_row * col_devs + src_col, dst_row * col_devs + dst_col))
    piece = lax.dynamic_slice_in_dim(row_panel, col_here * width, width, axis=0)
    piece = lax.ppermute(piece, ("frow", "fcol"), pairs)
    col_all = lax.all_gather(piece, "frow", axis=0, tiled=False)
    col_panel = (
        col_all.reshape(half, row_blocks, width, total)
        .transpose(1, 0, 2, 3)
        .reshape(local.shape[1], total)
    )
    rows_all = jnp.concatenate([row_panel, col_panel], axis=0).astype(jnp.float32)
    n_own = local.shape[0]
    full = lax.Precision.HIGHEST
    corner_blocks = total // width
    factor_full = jnp.zeros((total, total), jnp.float32)
    eye = jnp.eye(width, dtype=jnp.float32)
    inverses = []
    for h, cur in enumerate(halves):
        if h > 0:
            done_cols = factor_full[:, : h * split]
            cur = cur - jnp.dot(
                done_cols,
                done_cols[h * split : (h + 1) * split].T,
                precision=full,
                preferred_element_type=jnp.float32,
            )
        for b in range(split // width):
            start = h * split + b * width
            stop = start + width
            lb = b * width
            diag_block = cur[start:stop, lb : lb + width]
            symmetric = jnp.tril(diag_block) + jnp.tril(diag_block, -1).T
            factor = jnp.linalg.cholesky(symmetric)
            inverse = lax.linalg.triangular_solve(factor, eye, left_side=True, lower=True)
            inverses.append(inverse)
            factor_full = factor_full.at[start:stop, start:stop].set(factor)
            if stop < total:
                below = jnp.dot(
                    cur[stop:, lb : lb + width], inverse.T, precision=full, preferred_element_type=jnp.float32
                )
                factor_full = factor_full.at[stop:, start:stop].set(below)
                if lb + width < split:
                    cur = cur.at[stop:, lb + width :].add(
                        -jnp.dot(
                            below,
                            below[: split - lb - width].T,
                            precision=full,
                            preferred_element_type=jnp.float32,
                        )
                    )
    inv_blocks = jnp.stack(inverses)
    size = width
    while size < total:
        pairs_n = total // (2 * size)
        lower_left = jnp.stack(
            [
                factor_full[(2 * k + 1) * size : (2 * k + 2) * size, 2 * k * size : (2 * k + 1) * size]
                for k in range(pairs_n)
            ]
        )
        upper_inv = inv_blocks[0::2]
        lower_inv = inv_blocks[1::2]
        mixed = -jnp.einsum(
            "nab,nbc->nac",
            lower_inv,
            jnp.einsum("nab,nbc->nac", lower_left, upper_inv, precision=full),
            precision=full,
        )
        zeros = jnp.zeros_like(mixed)
        top = jnp.concatenate([upper_inv, zeros], axis=2)
        bottom = jnp.concatenate([mixed, lower_inv], axis=2)
        inv_blocks = jnp.concatenate([top, bottom], axis=1)
        size *= 2
    factor_inverse = inv_blocks[0]
    solved = jnp.dot(rows_all, factor_inverse.T, precision=hi, preferred_element_type=jnp.float32)
    row_factor = solved[:n_own]
    col_factor = solved[n_own:]
    corner_rows = lax.dynamic_slice_in_dim(
        factor_full, jnp.minimum(row_here, total // width - 1) * width, width, axis=0
    )
    head = jnp.where(row_here * width < total, corner_rows, row_factor[:width])
    panel_vals = jnp.concatenate([head, row_factor[width:]], axis=0)
    own_part = lax.dynamic_slice_in_dim(panel_vals, col_here * width, width, axis=1)
    result = lower_update(matrix, row_factor, col_factor, global_rows, global_cols, own_part)
    return result[None, :, None, :]


def solution(mesh):
    return jax.shard_map(
        shards,
        mesh=mesh,
        in_specs=(
            P("frow", None, "fcol", None),
            P(("frow", "fcol"), None, None),
            P(("frow", "fcol"), None),
            P(("frow", "fcol"), None),
            P(("frow", "fcol"), None),
        ),
        out_specs=P("frow", None, "fcol", None),
        check_vma=False,
    )
```
